256 devices in a mesh: tensor: 32 (over x_hi, z, core), rows: 8 (over x_lo, y).
Axes of the slice: x: 4 (x_hi: 2, x_lo: 2; x = x_hi * 2 + x_lo), y: 4, z: 8, core: 2. Of those that a mesh axis runs over, the one named last changes fastest.
Arguments:
- image: bfloat16 [64, 64, 3072], P('rows', None, 'tensor'), may hold values from -6 to 6
- dw_kernel: bfloat16 [7, 7, 3072], P(None, None, 'tensor'), may hold values from -0.875 to 0.875
- dw_bias: float32 [3072], P('tensor'), may hold values from -3 to 3
- norm_gain: float32 [3072], replicated, may hold values from 0.1 to 1.9
- norm_bias: float32 [3072], replicated, may hold values from -2 to 2
- w_expand: bfloat16 [3072, 12288], P('rows', 'tensor'), may hold values from -0.21875 to 0.21875
- b_expand: float32 [12288], P('tensor'), may hold values from -3 to 3
- w_project: bfloat16 [12288, 3072], P('tensor', 'rows'), may hold values from -0.109375 to 0.109375
- b_project: float32 [3072], P('tensor'), may hold values from -3 to 3
- layer_scale: float32 [3072], P('tensor'), may hold values from 0.25 to 2
- out_grad: bfloat16 [64, 64, 3072], P('rows', None, 'tensor'), may hold values from -6 to 6
Outputs:
- result: bfloat16 [64, 64, 3072], P('rows', None, 'tensor')
- image_grad: bfloat16 [64, 64, 3072], P('rows', None, 'tensor')
- expand_grad: float32 [3072, 12288], P('rows', 'tensor')
- project_grad: float32 [12288, 3072], P('tensor', 'rows')
- kernel_grad: float32 [7, 7, 3072], P(None, None, 'tensor')
- scale_grad: float32 [3072], P('tensor')
The draws below stay inside these ranges and needn't reach their ends.
All inputs are finite; a program needn't handle non-finite values.
Results may differ from the reference program's by a relative error of at most 0.022.
Values may be sent and summed in bfloat16 or wider, within the bound.
No kernel may reach another device: no remote copies, remote signals or barrier semaphores. Data moves between devices by JAX's collectives and lax.ppermute only.
A program may use at most 128 MiB of HBM per device.

```python
import math
import jax
import jax.numpy as jnp
from jax import lax

D = 3072
FF = 12288
KS = 7
IMG_W = 64
HEIGHT = 64
N_TENSOR = 32


def spiked(entries, rng, source, target, blocks, factor):
    owner, partner = [(jnp.arange(entries.shape[axis_at]) // (entries.shape[axis_at] // blocks)).reshape([-1 if axis == axis_at else 1 for axis in range(entries.ndim)]) for axis_at in (source, target)]
    chosen = jax.random.permutation(rng, blocks)[partner]
    strong = (owner == chosen) | (owner == (partner + blocks // 2) % blocks)
    return jnp.where(strong, factor * entries, entries)


def block_levels(rng, shape, shards, low, top_value):
    level = 1.0
    for dim, shards_of in shards:
        heights = jax.random.uniform(jax.random.fold_in(jax.random.fold_in(rng, 6), dim), (shards_of,), jnp.float32, low / len(shards), top_value / len(shards))
        level = level * jnp.repeat(jnp.exp(heights), shape[dim] // shards_of).reshape((-1,) + (1,) * (len(shape) - 1 - dim))
    return level


def noise(rng, dims, width, limit, cuts=(), dtype=jnp.bfloat16):
    drawn = width * jax.random.normal(rng, dims, jnp.float32)
    if cuts:
        drawn = drawn * block_levels(rng, dims, cuts, -0.22, 0.18)
    return jnp.clip(drawn, -limit, limit).astype(dtype)


def gaussian_with(key, extent, spread, bound, shards, heavy, kind=jnp.bfloat16):
    entries = spread * jax.random.normal(key, extent, jnp.float32)
    if shards:
        entries = entries * block_levels(key, extent, shards, -0.22, 0.18)
    return jnp.clip(spiked(entries, jax.random.fold_in(key, 3), *heavy), -bound, bound).astype(kind)


def setup_inputs(seed: int = 0) -> dict:
    arg_keys = jax.random.split(jax.random.key(seed), 12)
    image = noise(arg_keys[0], (HEIGHT, IMG_W, D), 1.0, 6.0, ((0, 8), (2, 32)))
    dw_kernel = noise(arg_keys[1], (KS, KS, D), (KS * KS) ** -0.5, 0.875, ((2, 32),))
    dw_bias = noise(arg_keys[2], (D,), 0.5, 3.0, ((0, 32),), jnp.float32)
    norm_gain = jnp.clip(1.0 + 0.18 * jax.random.normal(arg_keys[3], (D,), jnp.float32), 0.1, 1.9)
    norm_bias = noise(arg_keys[4], (D,), 0.3, 2.0, (), jnp.float32)
    w_expand = gaussian_with(arg_keys[5], (D, FF), D ** -0.5, 0.21875, ((0, 8), (1, 32)), (1, 0, 32, 2.75))
    b_expand = noise(arg_keys[6], (FF,), 0.5, 3.0, ((0, 32),), jnp.float32)
    w_project = gaussian_with(arg_keys[7], (FF, D), FF ** -0.5, 0.109375, ((0, 32), (1, 8)), (0, 1, 32, 2.75))
    b_project = noise(arg_keys[8], (D,), 0.5, 3.0, ((0, 32),), jnp.float32)
    layer_scale = jnp.clip(jnp.exp(math.log(2.0) - 2.0794415 * jax.random.uniform(arg_keys[9], (D,), jnp.float32) ** block_levels(arg_keys[9], (D,), ((0, 32),), -0.2, 0.2)), 0.25, 2.0)
    out_grad = noise(arg_keys[10], (HEIGHT, IMG_W, D), 1.0, 6.0, ((0, 8), (2, 32)))
    return dict(image=image, dw_kernel=dw_kernel, dw_bias=dw_bias, norm_gain=norm_gain, norm_bias=norm_bias, w_expand=w_expand, b_expand=b_expand, w_project=w_project, b_project=b_project, layer_scale=layer_scale, out_grad=out_grad)


EPSILON = 1e-06

def gelu_exact(values):
    return 0.5 * values * (1.0 + lax.erf(values * (1.0 / math.sqrt(2.0))))

def gelu_slope(values):
    cumulative = 0.5 * (1.0 + lax.erf(values * (1.0 / math.sqrt(2.0))))
    density = jnp.exp(-0.5 * values * values) * (1.0 / math.sqrt(2.0 * math.pi))
    return cumulative + values * density

def depthwise(padded, kernel, height, breadth):
    kernel_size = kernel.shape[0]
    summed = jnp.zeros((height, breadth, kernel.shape[2]), jnp.float32)
    for row_shift in range(kernel_size):
        for col_shift in range(kernel_size):
            window = padded[row_shift:row_shift + height, col_shift:col_shift + breadth]
            summed = summed + kernel[row_shift, col_shift].astype(jnp.float32) * window
    return summed

def kernel_terms(padded, gradient, kernel_size):
    height, breadth = (gradient.shape[0], gradient.shape[1])
    kernel_rows = []
    for row_shift in range(kernel_size):
        kernel_line = []
        for col_shift in range(kernel_size):
            window = padded[row_shift:row_shift + height, col_shift:col_shift + breadth]
            kernel_line.append(lax.optimization_barrier(jnp.sum(window * gradient, axis=(0, 1))))
        kernel_rows.append(jnp.stack(kernel_line))
    return jnp.stack(kernel_rows)

def grouped_product(left, right):
    groups = N_TENSOR
    span = left.shape[1] // groups
    left_blocks = jnp.transpose(left.reshape(left.shape[0], groups, span), (1, 0, 2))
    right_blocks = right.reshape(groups, span, right.shape[1])

    def add_group(summed, blocks):
        term = jnp.dot(blocks[0], blocks[1], preferred_element_type=jnp.float32)
        rounded = lax.optimization_barrier(term.astype(jnp.bfloat16))
        return (summed + rounded.astype(jnp.float32), None)
    start = jnp.zeros((left.shape[0], right.shape[1]), jnp.float32)
    summed, unused = lax.scan(add_group, start, (left_blocks, right_blocks))
    return summed

def reference(image, dw_kernel, dw_bias, norm_gain, norm_bias, w_expand, b_expand, w_project, b_project, layer_scale, out_grad):
    height, breadth, features = image.shape
    positions = height * breadth
    rim_depth = dw_kernel.shape[0] // 2
    padded_image = jnp.pad(image.astype(jnp.float32), ((rim_depth, rim_depth), (rim_depth, rim_depth), (0, 0)))
    convolved = depthwise(padded_image, dw_kernel, height, breadth) + dw_bias
    mixed = convolved.astype(jnp.bfloat16).reshape(positions, features).astype(jnp.float32)
    average = lax.optimization_barrier(jnp.sum(mixed, 1, keepdims=True)) / features
    mean_square = lax.optimization_barrier(jnp.sum(mixed * mixed, 1, keepdims=True)) / features
    inv_std = lax.rsqrt(mean_square - average * average + EPSILON)
    centred = (mixed - average) * inv_std
    normed = (centred * norm_gain + norm_bias).astype(jnp.bfloat16)
    pre = jnp.dot(normed, w_expand, preferred_element_type=jnp.float32) + b_expand
    hidden = gelu_exact(pre).astype(jnp.bfloat16)
    projected = grouped_product(hidden, w_project) + b_project
    residual = image.reshape(positions, features).astype(jnp.float32)
    result = (residual + layer_scale * projected).astype(jnp.bfloat16).reshape(height, breadth, features)
    upstream = out_grad.reshape(positions, features).astype(jnp.float32)
    scale_grad = lax.optimization_barrier(jnp.sum(upstream * projected, 0))
    scaled_grad = (upstream * layer_scale).astype(jnp.bfloat16)
    project_grad = jnp.dot(hidden.T, scaled_grad, preferred_element_type=jnp.float32)
    hidden_grad = jnp.dot(scaled_grad, w_project.T, preferred_element_type=jnp.float32)
    pre_grad = (hidden_grad * gelu_slope(pre)).astype(jnp.bfloat16)
    expand_grad = jnp.dot(normed.T, pre_grad, preferred_element_type=jnp.float32)
    normed_grad = grouped_product(pre_grad, w_expand.T)
    gain_grad = normed_grad * norm_gain
    plain_mean = lax.optimization_barrier(jnp.sum(gain_grad, 1, keepdims=True)) / features
    centred_mean = lax.optimization_barrier(jnp.sum(gain_grad * centred, 1, keepdims=True)) / features
    mixed_grad = (inv_std * (gain_grad - plain_mean - centred * centred_mean)).astype(jnp.bfloat16)
    mixed_grad = mixed_grad.reshape(height, breadth, features).astype(jnp.float32)
    padded_grad = jnp.pad(mixed_grad, ((rim_depth, rim_depth), (rim_depth, rim_depth), (0, 0)))
    back = depthwise(padded_grad, dw_kernel[::-1, ::-1], height, breadth)
    image_grad = (upstream.reshape(height, breadth, features) + back).astype(jnp.bfloat16)
    kernel_grad = kernel_terms(padded_image, mixed_grad, dw_kernel.shape[0])
    return (result, image_grad, expand_grad, project_grad, kernel_grad, scale_grad)
```

```python
import math

import jax
import jax.numpy as jnp
from jax import lax
from jax.sharding import Mesh
from jax.sharding import PartitionSpec as P

EPSILON = 1e-06

TENSOR = ("xh", "z", "c")
ROWS = ("xl", "y")


def shifted(x, axis, count, step):
    return lax.ppermute(x, axis, [(i, (i + step) % count) for i in range(count)])


def order2(mine, other, index):
    first = jnp.where(index == 0, mine, other)
    second = jnp.where(index == 0, other, mine)
    return jnp.stack([first, second])


def ring_gather(x, axis, count):
    me = lax.axis_index(axis)
    ahead = count // 2
    behind = count - 1 - ahead
    rel = {0: x}
    fwd = x
    for s in range(1, ahead + 1):
        fwd = shifted(fwd, axis, count, 1)
        rel[-s] = fwd
    bwd = x
    for s in range(1, behind + 1):
        bwd = shifted(bwd, axis, count, -1)
        rel[s] = bwd
    stacked = jnp.stack([rel[k] if k <= behind else rel[k - count] for k in range(count)])
    doubled = jnp.concatenate([stacked, stacked])
    return lax.dynamic_slice_in_dim(doubled, (count - me) % count, count, axis=0)


def ring_scatter(blocks, axis, count, send_dtype):
    me = lax.axis_index(axis)

    def block(k):
        return lax.dynamic_index_in_dim(blocks, (me + k + count) % count, axis=0, keepdims=False).astype(
            jnp.float32
        )

    ahead = count // 2
    behind = count - 1 - ahead
    total = block(0)
    acc = None
    for s in range(1, ahead + 1):
        part = block(ahead + 1 - s)
        part = part if acc is None else acc + part
        acc = shifted(part.astype(send_dtype), axis, count, 1).astype(jnp.float32)
    total = total + acc
    acc = None
    for s in range(1, behind + 1):
        part = block(-(behind + 1 - s))
        part = part if acc is None else acc + part
        acc = shifted(part.astype(send_dtype), axis, count, -1).astype(jnp.float32)
    if acc is not None:
        total = total + acc
    return total


def gather_channels(x):
    core = lax.axis_index("c")
    far = lax.axis_index("xh")
    positions, width = x.shape
    half = positions // 2
    own = lax.dynamic_slice_in_dim(x, core * half, half, axis=0)
    sent = lax.dynamic_slice_in_dim(x, (1 - core) * half, half, axis=0)
    chip = order2(own, shifted(sent, "c", 2, 1), core)
    chip = jnp.transpose(chip, (1, 0, 2)).reshape(half, 2 * width)
    pair = order2(chip, shifted(chip, "xh", 2, 1), far)
    pair = jnp.transpose(pair, (1, 0, 2))
    ring = ring_gather(pair, "z", lax.axis_size("z"))
    ring = jnp.transpose(ring, (1, 2, 0, 3)).reshape(half, -1)
    both = order2(ring, shifted(ring, "c", 2, 1), core)
    return both.reshape(positions, -1)


def scatter_channels(partial):
    core = lax.axis_index("c")
    far = lax.axis_index("xh")
    zs = lax.axis_size("z")
    positions, features = partial.shape
    half = positions // 2
    width = features // (4 * zs)
    own = lax.dynamic_slice_in_dim(partial, core * half, half, axis=0)
    sent = lax.dynamic_slice_in_dim(partial, (1 - core) * half, half, axis=0)
    chip = own.astype(jnp.float32) + shifted(sent, "c", 2, 1).astype(jnp.float32)
    blocks = jnp.transpose(chip.reshape(half, 2, zs, 2, width), (2, 0, 1, 3, 4))
    ring = ring_scatter(blocks, "z", zs, jnp.bfloat16)
    mine = lax.dynamic_index_in_dim(ring, far, axis=1, keepdims=False)
    theirs = lax.dynamic_index_in_dim(ring, 1 - far, axis=1, keepdims=False)
    pair = mine + shifted(theirs.astype(jnp.bfloat16), "xh", 2, 1).astype(jnp.float32)
    keep = lax.dynamic_index_in_dim(pair, core, axis=1, keepdims=False)
    give = lax.dynamic_index_in_dim(pair, 1 - core, axis=1, keepdims=False)
    both = order2(keep, shifted(give, "c", 2, 1), core)
    return both.reshape(positions, width)


def gather_rows(w, dim, y_first):
    ys = lax.axis_size("y")
    w = jnp.moveaxis(w, dim, 0)
    if y_first:
        g = ring_gather(w, "y", ys)
        g = ring_gather(g, "xl", 2)
    else:
        g = ring_gather(w, "xl", 2)
        g = ring_gather(g, "y", ys)
        g = jnp.swapaxes(g, 0, 1)
    g = g.reshape((-1,) + w.shape[1:])
    return jnp.moveaxis(g, 0, dim)


def scatter_rows(term, dim, y_first):
    ys = lax.axis_size("y")
    term = jnp.moveaxis(term, dim, 0)
    rest = term.shape[1:]
    block = term.shape[0] // (2 * ys)
    term = term.reshape((2, ys, block) + rest)
    if y_first:
        part = ring_scatter(jnp.swapaxes(term, 0, 1), "y", ys, jnp.bfloat16)
        part = ring_scatter(part, "xl", 2, jnp.bfloat16)
    else:
        part = ring_scatter(term, "xl", 2, jnp.bfloat16)
        part = ring_scatter(part, "y", ys, jnp.bfloat16)
    return jnp.moveaxis(part, 0, dim)


def sum_tensor(v):
    v = v + shifted(v, "c", 2, 1)
    v = v + shifted(v, "xh", 2, 1)
    return jnp.sum(ring_gather(v, "z", lax.axis_size("z")), axis=0)


def sum_rows(v):
    v = v + shifted(v, "xl", 2, 1)
    return jnp.sum(ring_gather(v, "y", lax.axis_size("y")), axis=0)


def extended(cells, width):
    count = lax.axis_size(ROWS)
    ends = count - 1
    head = lax.slice_in_dim(cells, 0, width, axis=0)
    tail = lax.slice_in_dim(cells, cells.shape[0] - width, cells.shape[0], axis=0)
    return jnp.concatenate(
        [
            lax.ppermute(tail, ROWS, [(i, (i + 1) % count) for i in range(ends)]),
            cells,
            lax.ppermute(head, ROWS, [((i + 1) % count, i) for i in range(ends)]),
        ],
        axis=0,
    )


def gelu_exact(values):
    return 0.5 * values * (1.0 + lax.erf(values * (1.0 / math.sqrt(2.0))))


def gelu_slope(values):
    cumulative = 0.5 * (1.0 + lax.erf(values * (1.0 / math.sqrt(2.0))))
    density = jnp.exp(-0.5 * values * values) * (1.0 / math.sqrt(2.0 * math.pi))
    return cumulative + values * density


def depthwise(padded, kernel, height, breadth):
    kernel_size = kernel.shape[0]
    summed = jnp.zeros((height, breadth, kernel.shape[2]), jnp.float32)
    for row_shift in range(kernel_size):
        for col_shift in range(kernel_size):
            window = padded[row_shift : row_shift + height, col_shift : col_shift + breadth]
            summed = summed + kernel[row_shift, col_shift].astype(jnp.float32) * window
    return summed


def kernel_terms(padded, gradient, kernel_size):
    height, breadth = (gradient.shape[0], gradient.shape[1])
    kernel_rows = []
    for row_shift in range(kernel_size):
        kernel_line = []
        for col_shift in range(kernel_size):
            window = padded[row_shift : row_shift + height, col_shift : col_shift + breadth]
            kernel_line.append(jnp.sum(window * gradient, axis=(0, 1)))
        kernel_rows.append(jnp.stack(kernel_line))
    return jnp.stack(kernel_rows)


def contract_last(left, right):
    return lax.dot_general(
        left, right, (((1,), (1,)), ((), ())), preferred_element_type=jnp.float32
    )


def contract_first(left, right):
    return lax.dot_general(
        left, right, (((0,), (0,)), ((), ())), preferred_element_type=jnp.float32
    )


def per_device(
    image,
    dw_kernel,
    dw_bias,
    norm_gain,
    norm_bias,
    w_expand,
    b_expand,
    w_project,
    b_project,
    layer_scale,
    out_grad,
):
    kernel_size = dw_kernel.shape[0]
    rim_depth = kernel_size // 2
    height, breadth, channels = image.shape
    positions = height * breadth
    features = norm_gain.shape[0]
    channel_start = lax.axis_index(TENSOR) * channels

    w_expand_full = gather_rows(w_expand, 0, True)
    w_project_full = gather_rows(w_project, 1, False)
    upstream = out_grad.reshape(positions, channels).astype(jnp.float32)
    scaled_grad = (upstream * layer_scale).astype(jnp.bfloat16)
    grad_panels = gather_channels(scaled_grad)

    rimmed = extended(image, rim_depth)
    wide_image = jnp.pad(rimmed, ((0, 0), (rim_depth, rim_depth), (0, 0))).astype(jnp.float32)
    convolved = depthwise(wide_image, dw_kernel, height, breadth) + dw_bias
    mixed = convolved.astype(jnp.bfloat16).reshape(positions, channels)
    all_mixed = gather_channels(mixed).astype(jnp.float32)
    average = jnp.sum(all_mixed, 1, keepdims=True) / features
    mean_square = jnp.sum(all_mixed * all_mixed, 1, keepdims=True) / features
    inv_std = lax.rsqrt(mean_square - average * average + EPSILON)
    centred = (all_mixed - average) * inv_std
    normed = (centred * norm_gain + norm_bias).astype(jnp.bfloat16)
    pre = jnp.dot(normed, w_expand_full, preferred_element_type=jnp.float32) + b_expand
    hidden = gelu_exact(pre).astype(jnp.bfloat16)
    partial_out = jnp.dot(hidden, w_project_full, preferred_element_type=jnp.float32)
    projected = scatter_channels(partial_out.astype(jnp.bfloat16)) + b_project
    residual = image.reshape(positions, channels).astype(jnp.float32)
    result = (
        (residual + layer_scale * projected).astype(jnp.bfloat16).reshape(height, breadth, channels)
    )
    scale_term = jnp.sum(upstream * projected, 0)

    project_term = contract_first(hidden, grad_panels)
    project_grad = scatter_rows(project_term, 1, True)
    hidden_grad = contract_last(grad_panels, w_project_full)
    pre_grad = (hidden_grad * gelu_slope(pre)).astype(jnp.bfloat16)
    expand_grad = scatter_rows(contract_first(normed, pre_grad), 0, False)
    normed_partial = contract_last(pre_grad, w_expand_full).astype(jnp.bfloat16)
    gain_partial = normed_partial.astype(jnp.float32) * norm_gain
    stats = sum_tensor(jnp.stack([jnp.sum(gain_partial, 1), jnp.sum(gain_partial * centred, 1)]))
    normed_grad = scatter_channels(normed_partial)
    gain_part = lax.dynamic_slice_in_dim(norm_gain, channel_start, channels)
    centred_part = lax.dynamic_slice_in_dim(centred, channel_start, channels, axis=1)
    part_std = inv_std
    gain_grad = normed_grad * gain_part
    plain_mean = stats[0][:, None] / features
    centred_mean = stats[1][:, None] / features
    mixed_grad = (part_std * (gain_grad - plain_mean - centred_part * centred_mean)).astype(
        jnp.bfloat16
    )
    mixed_grad = mixed_grad.reshape(height, breadth, channels)
    grad_rimmed = extended(mixed_grad, rim_depth)
    wide_grad = jnp.pad(grad_rimmed, ((0, 0), (rim_depth, rim_depth), (0, 0))).astype(jnp.float32)
    back = depthwise(wide_grad, dw_kernel[::-1, ::-1], height, breadth)
    image_grad = (upstream.reshape(height, breadth, channels) + back).astype(jnp.bfloat16)
    kernel_local = kernel_terms(wide_image, mixed_grad.astype(jnp.float32), kernel_size)
    flat = sum_rows(jnp.concatenate([kernel_local.reshape(-1), scale_term]))
    kernel_grad = flat[: kernel_local.size].reshape(kernel_local.shape)
    scale_grad = flat[kernel_local.size :]
    return (result, image_grad, expand_grad, project_grad, kernel_grad, scale_grad)


def solution(mesh):
    tensor_size, rows_size = mesh.devices.shape
    far = 2
    core = 2
    near = 2
    fine = Mesh(
        mesh.devices.reshape(far, tensor_size // (far * core), core, near, rows_size // near),
        ("xh", "z", "c", "xl", "y"),
    )
    return jax.shard_map(
        per_device,
        mesh=fine,
        in_specs=(
            P(ROWS, None, TENSOR),
            P(None, None, TENSOR),
            P(TENSOR),
            P(),
            P(),
            P(ROWS, TENSOR),
            P(TENSOR),
            P(TENSOR, ROWS),
            P(TENSOR),
            P(TENSOR),
            P(ROWS, None, TENSOR),
        ),
        out_specs=(
            P(ROWS, None, TENSOR),
            P(ROWS, None, TENSOR),
            P(ROWS, TENSOR),
            P(TENSOR, ROWS),
            P(None, None, TENSOR),
            P(TENSOR),
        ),
        check_vma=False,
    )
```

```python
import math

import jax
import jax.numpy as jnp
from jax import lax
from jax.sharding import Mesh
from jax.sharding import PartitionSpec as P

EPSILON = 1e-06

TENSOR = ("xh", "z", "c")
ROWS = ("xl", "y")


def shifted(x, axis, count, step):
    return lax.ppermute(x, axis, [(i, (i + step) % count) for i in range(count)])


def order2(mine, other, index):
    first = jnp.where(index == 0, mine, other)
    second = jnp.where(index == 0, other, mine)
    return jnp.stack([first, second])


def ring_gather(x, axis, count):
    me = lax.axis_index(axis)
    ahead = count // 2
    behind = count - 1 - ahead
    rel = {0: x}
    fwd = x
    for s in range(1, ahead + 1):
        fwd = shifted(fwd, axis, count, 1)
        rel[-s] = fwd
    bwd = x
    for s in range(1, behind + 1):
        bwd = shifted(bwd, axis, count, -1)
        rel[s] = bwd
    stacked = jnp.stack([rel[k] if k <= behind else rel[k - count] for k in range(count)])
    doubled = jnp.concatenate([stacked, stacked])
    return lax.dynamic_slice_in_dim(doubled, (count - me) % count, count, axis=0)


def ring_scatter(blocks, axis, count, send_dtype):
    me = lax.axis_index(axis)

    def block(k):
        return lax.dynamic_index_in_dim(blocks, (me + k + count) % count, axis=0, keepdims=False).astype(
            jnp.float32
        )

    ahead = count // 2
    behind = count - 1 - ahead
    total = block(0)
    acc = None
    for s in range(1, ahead + 1):
        part = block(ahead + 1 - s)
        part = part if acc is None else acc + part
        acc = shifted(part.astype(send_dtype), axis, count, 1).astype(jnp.float32)
    total = total + acc
    acc = None
    for s in range(1, behind + 1):
        part = block(-(behind + 1 - s))
        part = part if acc is None else acc + part
        acc = shifted(part.astype(send_dtype), axis, count, -1).astype(jnp.float32)
    if acc is not None:
        total = total + acc
    return total


def gather_channels(x):
    core = lax.axis_index("c")
    far = lax.axis_index("xh")
    kinds, positions, width = x.shape
    half = positions // 2
    own = lax.dynamic_slice_in_dim(x, core * half, half, axis=1)
    sent = lax.dynamic_slice_in_dim(x, (1 - core) * half, half, axis=1)
    got = shifted(sent, "c", 2, 1)
    chip = jnp.concatenate(
        [jnp.where(core == 0, own, got), jnp.where(core == 0, got, own)], axis=2
    )
    other = shifted(chip, "xh", 2, 1)
    pair = jnp.stack(
        [jnp.where(far == 0, chip, other), jnp.where(far == 0, other, chip)], axis=2
    )
    ring = ring_gather(pair, "z", lax.axis_size("z"))
    ring = jnp.transpose(ring, (1, 2, 3, 0, 4)).reshape(kinds, half, -1)
    got = shifted(ring, "c", 2, 1)
    return jnp.concatenate(
        [jnp.where(core == 0, ring, got), jnp.where(core == 0, got, ring)], axis=1
    )


def scatter_channels(partial, extra):
    core = lax.axis_index("c")
    far = lax.axis_index("xh")
    zs = lax.axis_size("z")
    positions, features = partial.shape
    half = positions // 2
    width = features // (4 * zs)
    spread = jnp.broadcast_to(
        extra.astype(jnp.bfloat16)[:, None, None, None, :], (positions, 2, zs, 2, extra.shape[1])
    )
    partial = jnp.concatenate([partial.reshape(positions, 2, zs, 2, width), spread], axis=4)
    own = lax.dynamic_slice_in_dim(partial, core * half, half, axis=0)
    sent = lax.dynamic_slice_in_dim(partial, (1 - core) * half, half, axis=0)
    chip = own.astype(jnp.float32) + shifted(sent, "c", 2, 1).astype(jnp.float32)
    blocks = jnp.transpose(chip, (2, 0, 1, 3, 4))
    ring = ring_scatter(blocks, "z", zs, jnp.bfloat16)
    mine = lax.dynamic_index_in_dim(ring, far, axis=1, keepdims=False)
    theirs = lax.dynamic_index_in_dim(ring, 1 - far, axis=1, keepdims=False)
    pair = mine + shifted(theirs.astype(jnp.bfloat16), "xh", 2, 1).astype(jnp.float32)
    keep = lax.dynamic_index_in_dim(pair, core, axis=1, keepdims=False)
    give = lax.dynamic_index_in_dim(pair, 1 - core, axis=1, keepdims=False)
    got = shifted(give, "c", 2, 1)
    both = jnp.concatenate(
        [jnp.where(core == 0, keep, got), jnp.where(core == 0, got, keep)], axis=0
    )
    return both[:, :width], both[:, width:]


def gather_rows(w, dim):
    return lax.all_gather(w, ROWS, axis=dim, tiled=True)


def scatter_rows(term, dim):
    return lax.psum_scatter(
        term.astype(jnp.bfloat16), ROWS, scatter_dimension=dim, tiled=True
    ).astype(jnp.float32)


def sum_tensor(v):
    v = v + shifted(v, "c", 2, 1)
    v = v + shifted(v, "xh", 2, 1)
    return jnp.sum(ring_gather(v, "z", lax.axis_size("z")), axis=0)


def sum_rows(v):
    v = v + shifted(v, "xl", 2, 1)
    return jnp.sum(ring_gather(v, "y", lax.axis_size("y")), axis=0)


def extended(cells, width):
    count = lax.axis_size(ROWS)
    ends = count - 1
    head = lax.slice_in_dim(cells, 0, width, axis=0)
    tail = lax.slice_in_dim(cells, cells.shape[0] - width, cells.shape[0], axis=0)
    return jnp.concatenate(
        [
            lax.ppermute(tail, ROWS, [(i, (i + 1) % count) for i in range(ends)]),
            cells,
            lax.ppermute(head, ROWS, [((i + 1) % count, i) for i in range(ends)]),
        ],
        axis=0,
    )


def gelu_exact(values):
    return 0.5 * values * (1.0 + lax.erf(values * (1.0 / math.sqrt(2.0))))


def gelu_slope(values):
    cumulative = 0.5 * (1.0 + lax.erf(values * (1.0 / math.sqrt(2.0))))
    density = jnp.exp(-0.5 * values * values) * (1.0 / math.sqrt(2.0 * math.pi))
    return cumulative + values * density


def depthwise(padded, kernel, height, breadth):
    kernel_size = kernel.shape[0]
    summed = jnp.zeros((height, breadth, kernel.shape[2]), jnp.float32)
    for row_shift in range(kernel_size):
        for col_shift in range(kernel_size):
            window = padded[row_shift : row_shift + height, col_shift : col_shift + breadth]
            summed = summed + kernel[row_shift, col_shift].astype(jnp.float32) * window
    return summed


def kernel_terms(padded, gradient, kernel_size):
    height, breadth = (gradient.shape[0], gradient.shape[1])
    kernel_rows = []
    for row_shift in range(kernel_size):
        kernel_line = []
        for col_shift in range(kernel_size):
            window = padded[row_shift : row_shift + height, col_shift : col_shift + breadth]
            kernel_line.append(jnp.sum(window * gradient, axis=(0, 1)))
        kernel_rows.append(jnp.stack(kernel_line))
    return jnp.stack(kernel_rows)


def contract_last(left, right):
    return lax.dot_general(
        left, right, (((1,), (1,)), ((), ())), preferred_element_type=jnp.float32
    )


def contract_first(left, right):
    return lax.dot_general(
        left, right, (((0,), (0,)), ((), ())), preferred_element_type=jnp.float32
    )


def per_device(
    image,
    dw_kernel,
    dw_bias,
    norm_gain,
    norm_bias,
    w_expand,
    b_expand,
    w_project,
    b_project,
    layer_scale,
    out_grad,
):
    kernel_size = dw_kernel.shape[0]
    rim_depth = kernel_size // 2
    height, breadth, channels = image.shape
    positions = height * breadth
    features = norm_gain.shape[0]
    channel_start = lax.axis_index(TENSOR) * channels

    w_expand_full = gather_rows(w_expand, 0)
    w_project_full = gather_rows(w_project, 1)
    upstream = out_grad.reshape(positions, channels).astype(jnp.float32)
    scaled_grad = (upstream * layer_scale).astype(jnp.bfloat16)

    rimmed = extended(image, rim_depth)
    wide_image = jnp.pad(rimmed, ((0, 0), (rim_depth, rim_depth), (0, 0))).astype(jnp.float32)
    convolved = depthwise(wide_image, dw_kernel, height, breadth) + dw_bias
    mixed = convolved.astype(jnp.bfloat16).reshape(positions, channels)
    gathered = gather_channels(jnp.stack([mixed, scaled_grad]))
    all_mixed = gathered[0].astype(jnp.float32)
    grad_panels = gathered[1]
    average = jnp.sum(all_mixed, 1, keepdims=True) / features
    mean_square = jnp.sum(all_mixed * all_mixed, 1, keepdims=True) / features
    inv_std = lax.rsqrt(mean_square - average * average + EPSILON)
    centred = (all_mixed - average) * inv_std
    normed = (centred * norm_gain + norm_bias).astype(jnp.bfloat16)
    pre = jnp.dot(normed, w_expand_full, preferred_element_type=jnp.float32) + b_expand
    hidden = gelu_exact(pre).astype(jnp.bfloat16)
    partial_out = jnp.dot(hidden, w_project_full, preferred_element_type=jnp.float32)
    projected, _ = scatter_channels(partial_out.astype(jnp.bfloat16), jnp.zeros((positions, 0)))
    projected = projected + b_project
    residual = image.reshape(positions, channels).astype(jnp.float32)
    result = (
        (residual + layer_scale * projected).astype(jnp.bfloat16).reshape(height, breadth, channels)
    )
    scale_term = jnp.sum(upstream * projected, 0)

    project_term = contract_first(hidden, grad_panels)
    project_grad = scatter_rows(project_term, 1)
    hidden_grad = contract_last(grad_panels, w_project_full)
    pre_grad = (hidden_grad * gelu_slope(pre)).astype(jnp.bfloat16)
    expand_grad = scatter_rows(contract_first(normed, pre_grad), 0)
    normed_partial = contract_last(pre_grad, w_expand_full).astype(jnp.bfloat16)
    gain_partial = normed_partial.astype(jnp.float32) * norm_gain
    stat_partial = jnp.stack([jnp.sum(gain_partial, 1), jnp.sum(gain_partial * centred, 1)], axis=1)
    normed_grad, stats = scatter_channels(normed_partial, stat_partial)
    stats = stats.T
    gain_part = lax.dynamic_slice_in_dim(norm_gain, channel_start, channels)
    centred_part = lax.dynamic_slice_in_dim(centred, channel_start, channels, axis=1)
    part_std = inv_std
    gain_grad = normed_grad * gain_part
    plain_mean = stats[0][:, None] / features
    centred_mean = stats[1][:, None] / features
    mixed_grad = (part_std * (gain_grad - plain_mean - centred_part * centred_mean)).astype(
        jnp.bfloat16
    )
    mixed_grad = mixed_grad.reshape(height, breadth, channels)
    grad_rimmed = extended(mixed_grad, rim_depth)
    wide_grad = jnp.pad(grad_rimmed, ((0, 0), (rim_depth, rim_depth), (0, 0))).astype(jnp.float32)
    back = depthwise(wide_grad, dw_kernel[::-1, ::-1], height, breadth)
    image_grad = (upstream.reshape(height, breadth, channels) + back).astype(jnp.bfloat16)
    kernel_local = kernel_terms(wide_image, mixed_grad.astype(jnp.float32), kernel_size)
    flat = sum_rows(jnp.concatenate([kernel_local.reshape(-1), scale_term]))
    kernel_grad = flat[: kernel_local.size].reshape(kernel_local.shape)
    scale_grad = flat[kernel_local.size :]
    return (result, image_grad, expand_grad, project_grad, kernel_grad, scale_grad)


def solution(mesh):
    tensor_size, rows_size = mesh.devices.shape
    far = 2
    core = 2
    near = 2
    fine = Mesh(
        mesh.devices.reshape(far, tensor_size // (far * core), core, near, rows_size // near),
        ("xh", "z", "c", "xl", "y"),
    )
    return jax.shard_map(
        per_device,
        mesh=fine,
        in_specs=(
            P(ROWS, None, TENSOR),
            P(None, None, TENSOR),
            P(TENSOR),
            P(),
            P(),
            P(ROWS, TENSOR),
            P(TENSOR),
            P(TENSOR, ROWS),
            P(TENSOR),
            P(TENSOR),
            P(ROWS, None, TENSOR),
        ),
        out_specs=(
            P(ROWS, None, TENSOR),
            P(ROWS, None, TENSOR),
            P(ROWS, TENSOR),
            P(TENSOR, ROWS),
            P(None, None, TENSOR),
            P(TENSOR),
        ),
        check_vma=False,
    )
```

```python
import math

import jax
import jax.numpy as jnp
from jax import lax
from jax.sharding import Mesh
from jax.sharding import PartitionSpec as P

EPSILON = 1e-06

TENSOR = ("xh", "z", "c")
ROWS = ("xl", "y")


def shifted(x, axis, count, step):
    return lax.ppermute(x, axis, [(i, (i + step) % count) for i in range(count)])


def order2(mine, other, index):
    first = jnp.where(index == 0, mine, other)
    second = jnp.where(index == 0, other, mine)
    return jnp.stack([first, second])


def ring_gather(x, axis, count, out_axis=0):
    me = lax.axis_index(axis)
    ahead = count // 2
    behind = count - 1 - ahead
    rel = {0: x}
    fwd = x
    for s in range(1, ahead + 1):
        fwd = shifted(fwd, axis, count, 1)
        rel[-s] = fwd
    bwd = x
    for s in range(1, behind + 1):
        bwd = shifted(bwd, axis, count, -1)
        rel[s] = bwd
    placed = jnp.zeros(x.shape[:out_axis] + (count,) + x.shape[out_axis:], x.dtype)
    for k, part in rel.items():
        placed = lax.dynamic_update_index_in_dim(placed, part, (me + k + count) % count, out_axis)
    return placed


def ring_scatter(blocks, axis, count, send_dtype):
    me = lax.axis_index(axis)

    def block(k):
        return lax.dynamic_index_in_dim(blocks, (me + k + count) % count, axis=0, keepdims=False).astype(
            jnp.float32
        )

    ahead = count // 2
    behind = count - 1 - ahead
    total = block(0)
    acc = None
    for s in range(1, ahead + 1):
        part = block(ahead + 1 - s)
        part = part if acc is None else acc + part
        acc = shifted(part.astype(send_dtype), axis, count, 1).astype(jnp.float32)
    total = total + acc
    acc = None
    for s in range(1, behind + 1):
        part = block(-(behind + 1 - s))
        part = part if acc is None else acc + part
        acc = shifted(part.astype(send_dtype), axis, count, -1).astype(jnp.float32)
    if acc is not None:
        total = total + acc
    return total


def gather_channels(x):
    core = lax.axis_index("c")
    far = lax.axis_index("xh")
    kinds, positions, width = x.shape
    half = positions // 2
    own = lax.dynamic_slice_in_dim(x, core * half, half, axis=1)
    sent = lax.dynamic_slice_in_dim(x, (1 - core) * half, half, axis=1)
    got = shifted(sent, "c", 2, 1)
    chip = jnp.concatenate(
        [jnp.where(core == 0, own, got), jnp.where(core == 0, got, own)], axis=2
    )
    other = shifted(chip, "xh", 2, 1)
    pair = jnp.stack(
        [jnp.where(far == 0, chip, other), jnp.where(far == 0, other, chip)], axis=2
    )
    ring = ring_gather(pair, "z", lax.axis_size("z"), 3)
    ring = ring.reshape(kinds, half, -1)
    got = shifted(ring, "c", 2, 1)
    return jnp.concatenate(
        [jnp.where(core == 0, ring, got), jnp.where(core == 0, got, ring)], axis=1
    )


def scatter_channels(partial, extra):
    core = lax.axis_index("c")
    far = lax.axis_index("xh")
    zs = lax.axis_size("z")
    positions, features = partial.shape
    half = positions // 2
    width = features // (4 * zs)
    spread = jnp.broadcast_to(
        extra.astype(jnp.bfloat16)[:, None, None, None, :], (positions, 2, zs, 2, extra.shape[1])
    )
    partial = jnp.concatenate([partial.reshape(positions, 2, zs, 2, width), spread], axis=4)
    own = lax.dynamic_slice_in_dim(partial, core * half, half, axis=0)
    sent = lax.dynamic_slice_in_dim(partial, (1 - core) * half, half, axis=0)
    chip = own.astype(jnp.float32) + shifted(sent, "c", 2, 1).astype(jnp.float32)
    blocks = jnp.transpose(chip, (2, 0, 1, 3, 4))
    ring = ring_scatter(blocks, "z", zs, jnp.bfloat16)
    mine = lax.dynamic_index_in_dim(ring, far, axis=1, keepdims=False)
    theirs = lax.dynamic_index_in_dim(ring, 1 - far, axis=1, keepdims=False)
    pair = mine + shifted(theirs.astype(jnp.bfloat16), "xh", 2, 1).astype(jnp.float32)
    keep = lax.dynamic_index_in_dim(pair, core, axis=1, keepdims=False)
    give = lax.dynamic_index_in_dim(pair, 1 - core, axis=1, keepdims=False)
    got = shifted(give, "c", 2, 1)
    both = jnp.concatenate(
        [jnp.where(core == 0, keep, got), jnp.where(core == 0, got, keep)], axis=0
    )
    return both[:, :width], both[:, width:]


def gather_rows(w, dim, y_first):
    ys = lax.axis_size("y")
    if y_first:
        g = ring_gather(w, "y", ys, dim)
        g = ring_gather(g, "xl", 2, dim)
    else:
        g = ring_gather(w, "xl", 2, dim)
        g = ring_gather(g, "y", ys, dim + 1)
    shape = list(w.shape)
    shape[dim] *= 2 * ys
    return g.reshape(shape)


def scatter_rows(term, dim):
    return lax.psum_scatter(
        term.astype(jnp.bfloat16), ROWS, scatter_dimension=dim, tiled=True
    ).astype(jnp.float32)


def sum_rows(v):
    v = v + shifted(v, "xl", 2, 1)
    return jnp.sum(ring_gather(v, "y", lax.axis_size("y")), axis=0)


def extended(cells, width):
    count = lax.axis_size(ROWS)
    ends = count - 1
    head = lax.slice_in_dim(cells, 0, width, axis=0)
    tail = lax.slice_in_dim(cells, cells.shape[0] - width, cells.shape[0], axis=0)
    return jnp.concatenate(
        [
            lax.ppermute(tail, ROWS, [(i, (i + 1) % count) for i in range(ends)]),
            cells,
            lax.ppermute(head, ROWS, [((i + 1) % count, i) for i in range(ends)]),
        ],
        axis=0,
    )


def gelu_exact(values):
    return 0.5 * values * (1.0 + lax.erf(values * (1.0 / math.sqrt(2.0))))


def gelu_slope(values):
    cumulative = 0.5 * (1.0 + lax.erf(values * (1.0 / math.sqrt(2.0))))
    density = jnp.exp(-0.5 * values * values) * (1.0 / math.sqrt(2.0 * math.pi))
    return cumulative + values * density


def depthwise(padded, kernel, height, breadth):
    kernel_size = kernel.shape[0]
    summed = jnp.zeros((height, breadth, kernel.shape[2]), jnp.float32)
    for row_shift in range(kernel_size):
        for col_shift in range(kernel_size):
            window = padded[row_shift : row_shift + height, col_shift : col_shift + breadth]
            summed = summed + kernel[row_shift, col_shift].astype(jnp.float32) * window
    return summed


def kernel_terms(padded, gradient, kernel_size):
    height, breadth = (gradient.shape[0], gradient.shape[1])
    kernel_rows = []
    for row_shift in range(kernel_size):
        kernel_line = []
        for col_shift in range(kernel_size):
            window = padded[row_shift : row_shift + height, col_shift : col_shift + breadth]
            kernel_line.append(jnp.sum(window * gradient, axis=(0, 1)))
        kernel_rows.append(jnp.stack(kernel_line))
    return jnp.stack(kernel_rows)


def contract_last(left, right):
    return lax.dot_general(
        left, right, (((1,), (1,)), ((), ())), preferred_element_type=jnp.float32
    )


def contract_first(left, right):
    return lax.dot_general(
        left, right, (((0,), (0,)), ((), ())), preferred_element_type=jnp.float32
    )


def per_device(
    image,
    dw_kernel,
    dw_bias,
    norm_gain,
    norm_bias,
    w_expand,
    b_expand,
    w_project,
    b_project,
    layer_scale,
    out_grad,
):
    kernel_size = dw_kernel.shape[0]
    rim_depth = kernel_size // 2
    height, breadth, channels = image.shape
    positions = height * breadth
    features = norm_gain.shape[0]
    channel_start = lax.axis_index(TENSOR) * channels

    w_expand_full = gather_rows(w_expand, 0, True)
    w_project_full = gather_rows(w_project, 1, False)
    upstream = out_grad.reshape(positions, channels).astype(jnp.float32)
    scaled_grad = (upstream * layer_scale).astype(jnp.bfloat16)

    rimmed = extended(image, rim_depth)
    wide_image = jnp.pad(rimmed, ((0, 0), (rim_depth, rim_depth), (0, 0))).astype(jnp.float32)
    convolved = depthwise(wide_image, dw_kernel, height, breadth) + dw_bias
    mixed = convolved.astype(jnp.bfloat16).reshape(positions, channels)
    gathered = gather_channels(jnp.stack([mixed, scaled_grad]))
    all_mixed = gathered[0].astype(jnp.float32)
    grad_panels = gathered[1]
    average = jnp.sum(all_mixed, 1, keepdims=True) / features
    mean_square = jnp.sum(all_mixed * all_mixed, 1, keepdims=True) / features
    inv_std = lax.rsqrt(mean_square - average * average + EPSILON)
    centred = (all_mixed - average) * inv_std
    normed = (centred * norm_gain + norm_bias).astype(jnp.bfloat16)
    pre = jnp.dot(normed, w_expand_full, preferred_element_type=jnp.float32) + b_expand
    hidden = gelu_exact(pre).astype(jnp.bfloat16)
    partial_out = jnp.dot(hidden, w_project_full, preferred_element_type=jnp.float32)
    projected, _ = scatter_channels(partial_out.astype(jnp.bfloat16), jnp.zeros((positions, 0)))
    projected = projected + b_project
    residual = image.reshape(positions, channels).astype(jnp.float32)
    result = (
        (residual + layer_scale * projected).astype(jnp.bfloat16).reshape(height, breadth, channels)
    )
    scale_term = jnp.sum(upstream * projected, 0)

    project_term = contract_first(hidden, grad_panels)
    project_grad = scatter_rows(project_term, 1)
    hidden_grad = contract_last(grad_panels, w_project_full)
    pre_grad = (hidden_grad * gelu_slope(pre)).astype(jnp.bfloat16)
    expand_grad = scatter_rows(contract_first(normed, pre_grad), 0)
    normed_partial = contract_last(pre_grad, w_expand_full).astype(jnp.bfloat16)
    gain_partial = normed_partial.astype(jnp.float32) * norm_gain
    stat_partial = jnp.stack([jnp.sum(gain_partial, 1), jnp.sum(gain_partial * centred, 1)], axis=1)
    normed_grad, stats = scatter_channels(normed_partial, stat_partial)
    stats = stats.T
    gain_part = lax.dynamic_slice_in_dim(norm_gain, channel_start, channels)
    centred_part = lax.dynamic_slice_in_dim(centred, channel_start, channels, axis=1)
    part_std = inv_std
    gain_grad = normed_grad * gain_part
    plain_mean = stats[0][:, None] / features
    centred_mean = stats[1][:, None] / features
    mixed_grad = (part_std * (gain_grad - plain_mean - centred_part * centred_mean)).astype(
        jnp.bfloat16
    )
    mixed_grad = mixed_grad.reshape(height, breadth, channels)
    grad_rimmed = extended(mixed_grad, rim_depth)
    wide_grad = jnp.pad(grad_rimmed, ((0, 0), (rim_depth, rim_depth), (0, 0))).astype(jnp.float32)
    back = depthwise(wide_grad, dw_kernel[::-1, ::-1], height, breadth)
    image_grad = (upstream.reshape(height, breadth, channels) + back).astype(jnp.bfloat16)
    kernel_local = kernel_terms(wide_image, mixed_grad.astype(jnp.float32), kernel_size)
    flat = sum_rows(jnp.concatenate([kernel_local.reshape(-1), scale_term]))
    kernel_grad = flat[: kernel_local.size].reshape(kernel_local.shape)
    scale_grad = flat[kernel_local.size :]
    return (result, image_grad, expand_grad, project_grad, kernel_grad, scale_grad)


def solution(mesh):
    tensor_size, rows_size = mesh.devices.shape
    far = 2
    core = 2
    near = 2
    fine = Mesh(
        mesh.devices.reshape(far, tensor_size // (far * core), core, near, rows_size // near),
        ("xh", "z", "c", "xl", "y"),
    )
    return jax.shard_map(
        per_device,
        mesh=fine,
        in_specs=(
            P(ROWS, None, TENSOR),
            P(None, None, TENSOR),
            P(TENSOR),
            P(),
            P(),
            P(ROWS, TENSOR),
            P(TENSOR),
            P(TENSOR, ROWS),
            P(TENSOR),
            P(TENSOR),
            P(ROWS, None, TENSOR),
        ),
        out_specs=(
            P(ROWS, None, TENSOR),
            P(ROWS, None, TENSOR),
            P(ROWS, TENSOR),
            P(TENSOR, ROWS),
            P(None, None, TENSOR),
            P(TENSOR),
        ),
        check_vma=False,
    )
```

```python
import math

import jax
import jax.numpy as jnp
from jax import lax
from jax.sharding import Mesh
from jax.sharding import PartitionSpec as P

EPSILON = 1e-06

TENSOR = ("xh", "z", "c")
ROWS = ("xl", "y")


def shifted(x, axis, count, step):
    return lax.ppermute(x, axis, [(i, (i + step) % count) for i in range(count)])


def order2(mine, other, index):
    first = jnp.where(index == 0, mine, other)
    second = jnp.where(index == 0, other, mine)
    return jnp.stack([first, second])


def ring_gather(x, axis, count, out_axis=0):
    me = lax.axis_index(axis)
    ahead = count // 2
    behind = count - 1 - ahead
    rel = {0: x}
    fwd = x
    for s in range(1, ahead + 1):
        fwd = shifted(fwd, axis, count, 1)
        rel[-s] = fwd
    bwd = x
    for s in range(1, behind + 1):
        bwd = shifted(bwd, axis, count, -1)
        rel[s] = bwd
    placed = jnp.zeros(x.shape[:out_axis] + (count,) + x.shape[out_axis:], x.dtype)
    for k, part in rel.items():
        placed = lax.dynamic_update_index_in_dim(placed, part, (me + k + count) % count, out_axis)
    return placed


def ring_scatter(blocks, axis, count, send_dtype):
    me = lax.axis_index(axis)

    def block(k):
        return lax.dynamic_index_in_dim(blocks, (me + k + count) % count, axis=0, keepdims=False).astype(
            jnp.float32
        )

    ahead = count // 2
    behind = count - 1 - ahead
    total = block(0)
    acc = None
    for s in range(1, ahead + 1):
        part = block(ahead + 1 - s)
        part = part if acc is None else acc + part
        acc = shifted(part.astype(send_dtype), axis, count, 1).astype(jnp.float32)
    total = total + acc
    acc = None
    for s in range(1, behind + 1):
        part = block(-(behind + 1 - s))
        part = part if acc is None else acc + part
        acc = shifted(part.astype(send_dtype), axis, count, -1).astype(jnp.float32)
    if acc is not None:
        total = total + acc
    return total


def gather_channels(x):
    core = lax.axis_index("c")
    far = lax.axis_index("xh")
    kinds, positions, width = x.shape
    half = positions // 2
    own = lax.dynamic_slice_in_dim(x, core * half, half, axis=1)
    sent = lax.dynamic_slice_in_dim(x, (1 - core) * half, half, axis=1)
    got = shifted(sent, "c", 2, 1)
    chip = jnp.concatenate(
        [jnp.where(core == 0, own, got), jnp.where(core == 0, got, own)], axis=2
    )
    other = shifted(chip, "xh", 2, 1)
    pair = jnp.stack(
        [jnp.where(far == 0, chip, other), jnp.where(far == 0, other, chip)], axis=2
    )
    ring = ring_gather(pair, "z", lax.axis_size("z"), 3)
    return ring.reshape(kinds, half, -1)


def scatter_channels(chip, extra):
    core = lax.axis_index("c")
    far = lax.axis_index("xh")
    zs = lax.axis_size("z")
    half, features = chip.shape
    width = features // (4 * zs)
    spread = jnp.broadcast_to(
        extra.astype(jnp.float32)[:, None, None, None, :], (half, 2, zs, 2, extra.shape[1])
    )
    chip = jnp.concatenate([chip.astype(jnp.float32).reshape(half, 2, zs, 2, width), spread], axis=4)
    blocks = jnp.transpose(chip, (2, 0, 1, 3, 4))
    ring = ring_scatter(blocks, "z", zs, jnp.bfloat16)
    mine = lax.dynamic_index_in_dim(ring, far, axis=1, keepdims=False)
    theirs = lax.dynamic_index_in_dim(ring, 1 - far, axis=1, keepdims=False)
    pair = mine + shifted(theirs.astype(jnp.bfloat16), "xh", 2, 1).astype(jnp.float32)
    keep = lax.dynamic_index_in_dim(pair, core, axis=1, keepdims=False)
    give = lax.dynamic_index_in_dim(pair, 1 - core, axis=1, keepdims=False)
    both = by_core(keep, shifted(give, "c", 2, 1), 0)
    return both[:, :width], both[:, width:]


def by_core(mine, other, axis):
    core = lax.axis_index("c")
    return jnp.concatenate(
        [jnp.where(core == 0, mine, other), jnp.where(core == 0, other, mine)], axis=axis
    )


def chip_blocks(x, axis):
    return by_core(x, shifted(x, "c", 2, 1), axis)


def fold_cores(term, axis):
    core = lax.axis_index("c")
    size = term.shape[axis] // 2
    mine = lax.dynamic_slice_in_dim(term, core * size, size, axis=axis)
    give = lax.dynamic_slice_in_dim(term, (1 - core) * size, size, axis=axis)
    return mine + shifted(give.astype(jnp.bfloat16), "c", 2, 1).astype(jnp.float32)


def gather_rows(w, dim):
    return lax.all_gather(w, ROWS, axis=dim, tiled=True)


def scatter_rows(term, dim):
    return lax.psum_scatter(
        term.astype(jnp.bfloat16), ROWS, scatter_dimension=dim, tiled=True
    ).astype(jnp.float32)


def sum_rows(v):
    v = v + shifted(v, "xl", 2, 1)
    return jnp.sum(ring_gather(v, "y", lax.axis_size("y")), axis=0)


def extended(cells, width):
    count = lax.axis_size(ROWS)
    ends = count - 1
    head = lax.slice_in_dim(cells, 0, width, axis=0)
    tail = lax.slice_in_dim(cells, cells.shape[0] - width, cells.shape[0], axis=0)
    return jnp.concatenate(
        [
            lax.ppermute(tail, ROWS, [(i, (i + 1) % count) for i in range(ends)]),
            cells,
            lax.ppermute(head, ROWS, [((i + 1) % count, i) for i in range(ends)]),
        ],
        axis=0,
    )


def gelu_exact(values):
    return 0.5 * values * (1.0 + lax.erf(values * (1.0 / math.sqrt(2.0))))


def gelu_slope(values):
    cumulative = 0.5 * (1.0 + lax.erf(values * (1.0 / math.sqrt(2.0))))
    density = jnp.exp(-0.5 * values * values) * (1.0 / math.sqrt(2.0 * math.pi))
    return cumulative + values * density


def depthwise(padded, kernel, height, breadth):
    kernel_size = kernel.shape[0]
    summed = jnp.zeros((height, breadth, kernel.shape[2]), jnp.float32)
    for row_shift in range(kernel_size):
        for col_shift in range(kernel_size):
            window = padded[row_shift : row_shift + height, col_shift : col_shift + breadth]
            summed = summed + kernel[row_shift, col_shift].astype(jnp.float32) * window
    return summed


def kernel_terms(padded, gradient, kernel_size):
    height, breadth = (gradient.shape[0], gradient.shape[1])
    kernel_rows = []
    for row_shift in range(kernel_size):
        kernel_line = []
        for col_shift in range(kernel_size):
            window = padded[row_shift : row_shift + height, col_shift : col_shift + breadth]
            kernel_line.append(jnp.sum(window * gradient, axis=(0, 1)))
        kernel_rows.append(jnp.stack(kernel_line))
    return jnp.stack(kernel_rows)


def contract_last(left, right):
    return lax.dot_general(
        left, right, (((1,), (1,)), ((), ())), preferred_element_type=jnp.float32
    )


def contract_first(left, right):
    return lax.dot_general(
        left, right, (((0,), (0,)), ((), ())), preferred_element_type=jnp.float32
    )


def per_device(
    image,
    dw_kernel,
    dw_bias,
    norm_gain,
    norm_bias,
    w_expand,
    b_expand,
    w_project,
    b_project,
    layer_scale,
    out_grad,
):
    kernel_size = dw_kernel.shape[0]
    rim_depth = kernel_size // 2
    height, breadth, channels = image.shape
    positions = height * breadth
    features = norm_gain.shape[0]
    channel_start = lax.axis_index(TENSOR) * channels

    core = lax.axis_index("c")
    half = positions // 2
    hidden_width = w_expand.shape[1]
    w_expand_chip = chip_blocks(gather_rows(w_expand, 0), 1)
    w_project_chip = chip_blocks(gather_rows(w_project, 1), 0)
    b_expand_chip = chip_blocks(b_expand, 0)
    upstream = out_grad.reshape(positions, channels).astype(jnp.float32)
    scaled_grad = (upstream * layer_scale).astype(jnp.bfloat16)

    rimmed = extended(image, rim_depth)
    wide_image = jnp.pad(rimmed, ((0, 0), (rim_depth, rim_depth), (0, 0))).astype(jnp.float32)
    convolved = depthwise(wide_image, dw_kernel, height, breadth) + dw_bias
    mixed = convolved.astype(jnp.bfloat16).reshape(positions, channels)
    gathered = gather_channels(jnp.stack([mixed, scaled_grad]))
    all_mixed = gathered[0].astype(jnp.float32)
    grad_panels = gathered[1]
    average = jnp.sum(all_mixed, 1, keepdims=True) / features
    mean_square = jnp.sum(all_mixed * all_mixed, 1, keepdims=True) / features
    inv_std = lax.rsqrt(mean_square - average * average + EPSILON)
    centred = (all_mixed - average) * inv_std
    normed = (centred * norm_gain + norm_bias).astype(jnp.bfloat16)
    pre = jnp.dot(normed, w_expand_chip, preferred_element_type=jnp.float32) + b_expand_chip
    hidden = gelu_exact(pre).astype(jnp.bfloat16)
    partial_out = sum(
        jnp.dot(
            hidden[:, g * hidden_width : (g + 1) * hidden_width],
            w_project_chip[g * hidden_width : (g + 1) * hidden_width],
            preferred_element_type=jnp.float32,
        )
        .astype(jnp.bfloat16)
        .astype(jnp.float32)
        for g in range(2)
    )
    projected, _ = scatter_channels(partial_out, jnp.zeros((half, 0)))
    projected = projected + b_project
    residual = image.reshape(positions, channels).astype(jnp.float32)
    result = (
        (residual + layer_scale * projected).astype(jnp.bfloat16).reshape(height, breadth, channels)
    )
    scale_term = jnp.sum(upstream * projected, 0)

    project_term = fold_cores(contract_first(hidden, grad_panels), 0)
    project_grad = scatter_rows(project_term, 1)
    hidden_grad = contract_last(grad_panels, w_project_chip)
    pre_grad = (hidden_grad * gelu_slope(pre)).astype(jnp.bfloat16)
    expand_grad = scatter_rows(fold_cores(contract_first(normed, pre_grad), 1), 0)
    normed_partial = sum(
        contract_last(
            pre_grad[:, g * hidden_width : (g + 1) * hidden_width],
            w_expand_chip[:, g * hidden_width : (g + 1) * hidden_width],
        )
        .astype(jnp.bfloat16)
        .astype(jnp.float32)
        for g in range(2)
    )
    gain_partial = normed_partial * norm_gain
    stat_partial = jnp.stack([jnp.sum(gain_partial, 1), jnp.sum(gain_partial * centred, 1)], axis=1)
    normed_grad, stats = scatter_channels(normed_partial, stat_partial)
    stats = stats.T
    row_stats = chip_blocks(jnp.concatenate([average, inv_std], axis=1), 0)
    gain_part = lax.dynamic_slice_in_dim(norm_gain, channel_start, channels)
    centred_part = (mixed.astype(jnp.float32) - row_stats[:, :1]) * row_stats[:, 1:]
    part_std = row_stats[:, 1:]
    gain_grad = normed_grad * gain_part
    plain_mean = stats[0][:, None] / features
    centred_mean = stats[1][:, None] / features
    mixed_grad = (part_std * (gain_grad - plain_mean - centred_part * centred_mean)).astype(
        jnp.bfloat16
    )
    mixed_grad = mixed_grad.reshape(height, breadth, channels)
    grad_rimmed = extended(mixed_grad, rim_depth)
    wide_grad = jnp.pad(grad_rimmed, ((0, 0), (rim_depth, rim_depth), (0, 0))).astype(jnp.float32)
    back = depthwise(wide_grad, dw_kernel[::-1, ::-1], height, breadth)
    image_grad = (upstream.reshape(height, breadth, channels) + back).astype(jnp.bfloat16)
    kernel_local = kernel_terms(wide_image, mixed_grad.astype(jnp.float32), kernel_size)
    flat = sum_rows(jnp.concatenate([kernel_local.reshape(-1), scale_term]))
    kernel_grad = flat[: kernel_local.size].reshape(kernel_local.shape)
    scale_grad = flat[kernel_local.size :]
    return (result, image_grad, expand_grad, project_grad, kernel_grad, scale_grad)


def solution(mesh):
    tensor_size, rows_size = mesh.devices.shape
    far = 2
    core = 2
    near = 2
    fine = Mesh(
        mesh.devices.reshape(far, tensor_size // (far * core), core, near, rows_size // near),
        ("xh", "z", "c", "xl", "y"),
    )
    return jax.shard_map(
        per_device,
        mesh=fine,
        in_specs=(
            P(ROWS, None, TENSOR),
            P(None, None, TENSOR),
            P(TENSOR),
            P(),
            P(),
            P(ROWS, TENSOR),
            P(TENSOR),
            P(TENSOR, ROWS),
            P(TENSOR),
            P(TENSOR),
            P(ROWS, None, TENSOR),
        ),
        out_specs=(
            P(ROWS, None, TENSOR),
            P(ROWS, None, TENSOR),
            P(ROWS, TENSOR),
            P(TENSOR, ROWS),
            P(None, None, TENSOR),
            P(TENSOR),
        ),
        check_vma=False,
    )
```

```python
import math

import jax
import jax.numpy as jnp
from jax import lax
from jax.sharding import Mesh
from jax.sharding import PartitionSpec as P

EPSILON = 1e-06

TENSOR = ("xh", "z", "c")
ROWS = ("xl", "y")


def shifted(x, axis, count, step):
    return lax.ppermute(x, axis, [(i, (i + step) % count) for i in range(count)])


def order2(mine, other, index):
    first = jnp.where(index == 0, mine, other)
    second = jnp.where(index == 0, other, mine)
    return jnp.stack([first, second])


def ring_gather(x, axis, count, out_axis=0):
    me = lax.axis_index(axis)
    ahead = count // 2
    behind = count - 1 - ahead
    rel = {0: x}
    fwd = x
    for s in range(1, ahead + 1):
        fwd = shifted(fwd, axis, count, 1)
        rel[-s] = fwd
    bwd = x
    for s in range(1, behind + 1):
        bwd = shifted(bwd, axis, count, -1)
        rel[s] = bwd
    placed = jnp.zeros(x.shape[:out_axis] + (count,) + x.shape[out_axis:], x.dtype)
    for k, part in rel.items():
        placed = lax.dynamic_update_index_in_dim(placed, part, (me + k + count) % count, out_axis)
    return placed


def ring_scatter(blocks, axis, count, send_dtype):
    me = lax.axis_index(axis)

    def block(k):
        return lax.dynamic_index_in_dim(blocks, (me + k + count) % count, axis=0, keepdims=False).astype(
            jnp.float32
        )

    ahead = count // 2
    behind = count - 1 - ahead
    total = block(0)
    acc = None
    for s in range(1, ahead + 1):
        part = block(ahead + 1 - s)
        part = part if acc is None else acc + part
        acc = shifted(part.astype(send_dtype), axis, count, 1).astype(jnp.float32)
    total = total + acc
    acc = None
    for s in range(1, behind + 1):
        part = block(-(behind + 1 - s))
        part = part if acc is None else acc + part
        acc = shifted(part.astype(send_dtype), axis, count, -1).astype(jnp.float32)
    if acc is not None:
        total = total + acc
    return total


def gather_channels(x):
    core = lax.axis_index("c")
    far = lax.axis_index("xh")
    kinds, positions, width = x.shape
    half = positions // 2
    own = lax.dynamic_slice_in_dim(x, core * half, half, axis=1)
    sent = lax.dynamic_slice_in_dim(x, (1 - core) * half, half, axis=1)
    got = shifted(sent, "c", 2, 1)
    chip = jnp.concatenate(
        [jnp.where(core == 0, own, got), jnp.where(core == 0, got, own)], axis=2
    )
    other = shifted(chip, "xh", 2, 1)
    pair = jnp.stack(
        [jnp.where(far == 0, chip, other), jnp.where(far == 0, other, chip)], axis=2
    )
    ring = ring_gather(pair, "z", lax.axis_size("z"), 3)
    return ring.reshape(kinds, half, -1)


def scatter_channels(chip, extra):
    core = lax.axis_index("c")
    far = lax.axis_index("xh")
    zs = lax.axis_size("z")
    half, features = chip.shape
    width = features // (4 * zs)
    spread = jnp.broadcast_to(
        extra.astype(jnp.float32)[:, None, None, None, :], (half, 2, zs, 2, extra.shape[1])
    )
    chip = jnp.concatenate([chip.astype(jnp.float32).reshape(half, 2, zs, 2, width), spread], axis=4)
    blocks = jnp.transpose(chip, (2, 0, 1, 3, 4))
    ring = ring_scatter(blocks, "z", zs, jnp.bfloat16)
    mine = lax.dynamic_index_in_dim(ring, far, axis=1, keepdims=False)
    theirs = lax.dynamic_index_in_dim(ring, 1 - far, axis=1, keepdims=False)
    pair = mine + shifted(theirs.astype(jnp.bfloat16), "xh", 2, 1).astype(jnp.float32)
    keep = lax.dynamic_index_in_dim(pair, core, axis=1, keepdims=False)
    give = lax.dynamic_index_in_dim(pair, 1 - core, axis=1, keepdims=False)
    both = by_core(keep, shifted(give, "c", 2, 1), 0)
    return both[:, :width], both[:, width:]


def by_core(mine, other, axis):
    core = lax.axis_index("c")
    return jnp.concatenate(
        [jnp.where(core == 0, mine, other), jnp.where(core == 0, other, mine)], axis=axis
    )


def chip_blocks(x, axis):
    return by_core(x, shifted(x, "c", 2, 1), axis)


def fold_cores(term, axis):
    core = lax.axis_index("c")
    size = term.shape[axis] // 2
    mine = lax.dynamic_slice_in_dim(term, core * size, size, axis=axis)
    give = lax.dynamic_slice_in_dim(term, (1 - core) * size, size, axis=axis)
    return mine + shifted(give.astype(jnp.bfloat16), "c", 2, 1).astype(jnp.float32)


def gather_rows(w, dim):
    return lax.all_gather(w, ROWS, axis=dim, tiled=True)


def scatter_rows(term, dim):
    return lax.psum_scatter(
        term.astype(jnp.bfloat16), ROWS, scatter_dimension=dim, tiled=True
    ).astype(jnp.float32)


def sum_rows(v):
    v = v + shifted(v, "xl", 2, 1)
    return jnp.sum(ring_gather(v, "y", lax.axis_size("y")), axis=0)


def extended(cells, width):
    count = lax.axis_size(ROWS)
    ends = count - 1
    head = lax.slice_in_dim(cells, 0, width, axis=0)
    tail = lax.slice_in_dim(cells, cells.shape[0] - width, cells.shape[0], axis=0)
    return jnp.concatenate(
        [
            lax.ppermute(tail, ROWS, [(i, (i + 1) % count) for i in range(ends)]),
            cells,
            lax.ppermute(head, ROWS, [((i + 1) % count, i) for i in range(ends)]),
        ],
        axis=0,
    )


def gelu_exact(values):
    return 0.5 * values * (1.0 + lax.erf(values * (1.0 / math.sqrt(2.0))))


def gelu_slope(values):
    cumulative = 0.5 * (1.0 + lax.erf(values * (1.0 / math.sqrt(2.0))))
    density = jnp.exp(-0.5 * values * values) * (1.0 / math.sqrt(2.0 * math.pi))
    return cumulative + values * density


def depthwise(padded, kernel, height, breadth):
    kernel_size = kernel.shape[0]
    summed = jnp.zeros((height, breadth, kernel.shape[2]), jnp.float32)
    for row_shift in range(kernel_size):
        for col_shift in range(kernel_size):
            window = padded[row_shift : row_shift + height, col_shift : col_shift + breadth]
            summed = summed + kernel[row_shift, col_shift].astype(jnp.float32) * window
    return summed


def kernel_terms(padded, gradient, kernel_size):
    height, breadth = (gradient.shape[0], gradient.shape[1])
    kernel_rows = []
    for row_shift in range(kernel_size):
        kernel_line = []
        for col_shift in range(kernel_size):
            window = padded[row_shift : row_shift + height, col_shift : col_shift + breadth]
            kernel_line.append(jnp.sum(window * gradient, axis=(0, 1)))
        kernel_rows.append(jnp.stack(kernel_line))
    return jnp.stack(kernel_rows)


def contract_last(left, right):
    return lax.dot_general(
        left, right, (((1,), (1,)), ((), ())), preferred_element_type=jnp.float32
    )


def contract_first(left, right):
    return lax.dot_general(
        left, right, (((0,), (0,)), ((), ())), preferred_element_type=jnp.float32
    )


def per_device(
    image,
    dw_kernel,
    dw_bias,
    norm_gain,
    norm_bias,
    w_expand,
    b_expand,
    w_project,
    b_project,
    layer_scale,
    out_grad,
):
    kernel_size = dw_kernel.shape[0]
    rim_depth = kernel_size // 2
    height, breadth, channels = image.shape
    positions = height * breadth
    features = norm_gain.shape[0]
    channel_start = lax.axis_index(TENSOR) * channels

    core = lax.axis_index("c")
    half = positions // 2
    hidden_width = w_expand.shape[1]
    w_expand_chip = chip_blocks(gather_rows(w_expand, 0), 1)
    w_project_chip = chip_blocks(gather_rows(w_project, 1), 0)
    b_expand_chip = chip_blocks(b_expand, 0)
    upstream = out_grad.reshape(positions, channels).astype(jnp.float32)
    scaled_grad = (upstream * layer_scale).astype(jnp.bfloat16)

    rimmed = extended(image, rim_depth)
    wide_image = jnp.pad(rimmed, ((0, 0), (rim_depth, rim_depth), (0, 0))).astype(jnp.float32)
    convolved = depthwise(wide_image, dw_kernel, height, breadth) + dw_bias
    mixed = convolved.astype(jnp.bfloat16).reshape(positions, channels)
    gathered = gather_channels(jnp.stack([mixed, scaled_grad]))
    all_mixed = gathered[0].astype(jnp.float32)
    grad_panels = gathered[1]
    average = jnp.sum(all_mixed, 1, keepdims=True) / features
    mean_square = jnp.sum(all_mixed * all_mixed, 1, keepdims=True) / features
    inv_std = lax.rsqrt(mean_square - average * average + EPSILON)
    centred = (all_mixed - average) * inv_std
    normed = (centred * norm_gain + norm_bias).astype(jnp.bfloat16)
    pre = jnp.dot(normed, w_expand_chip, preferred_element_type=jnp.float32) + b_expand_chip
    hidden = gelu_exact(pre).astype(jnp.bfloat16)
    hidden_grad = contract_last(grad_panels, w_project_chip)
    pre_grad = (hidden_grad * gelu_slope(pre)).astype(jnp.bfloat16)
    normed_partial = sum(
        contract_last(
            pre_grad[:, g * hidden_width : (g + 1) * hidden_width],
            w_expand_chip[:, g * hidden_width : (g + 1) * hidden_width],
        )
        .astype(jnp.bfloat16)
        .astype(jnp.float32)
        for g in range(2)
    )
    gain_partial = normed_partial * norm_gain
    stat_partial = jnp.stack([jnp.sum(gain_partial, 1), jnp.sum(gain_partial * centred, 1)], axis=1)
    late_hidden, normed_partial, stat_partial = lax.optimization_barrier(
        (hidden, normed_partial, stat_partial)
    )
    normed_grad, stats = scatter_channels(normed_partial, stat_partial)
    stats = stats.T
    expand_grad = scatter_rows(fold_cores(contract_first(normed, pre_grad), 1), 0)
    project_term = fold_cores(contract_first(hidden, grad_panels), 0)
    project_grad = scatter_rows(project_term, 1)

    partial_out = sum(
        jnp.dot(
            late_hidden[:, g * hidden_width : (g + 1) * hidden_width],
            w_project_chip[g * hidden_width : (g + 1) * hidden_width],
            preferred_element_type=jnp.float32,
        )
        .astype(jnp.bfloat16)
        .astype(jnp.float32)
        for g in range(2)
    )
    projected, _ = scatter_channels(partial_out, jnp.zeros((half, 0)))
    projected = projected + b_project
    residual = image.reshape(positions, channels).astype(jnp.float32)
    result = (
        (residual + layer_scale * projected).astype(jnp.bfloat16).reshape(height, breadth, channels)
    )
    scale_term = jnp.sum(upstream * projected, 0)

    row_stats = chip_blocks(jnp.concatenate([average, inv_std], axis=1), 0)
    gain_part = lax.dynamic_slice_in_dim(norm_gain, channel_start, channels)
    centred_part = (mixed.astype(jnp.float32) - row_stats[:, :1]) * row_stats[:, 1:]
    part_std = row_stats[:, 1:]
    gain_grad = normed_grad * gain_part
    plain_mean = stats[0][:, None] / features
    centred_mean = stats[1][:, None] / features
    mixed_grad = (part_std * (gain_grad - plain_mean - centred_part * centred_mean)).astype(
        jnp.bfloat16
    )
    mixed_grad = mixed_grad.reshape(height, breadth, channels)
    grad_rimmed = extended(mixed_grad, rim_depth)
    wide_grad = jnp.pad(grad_rimmed, ((0, 0), (rim_depth, rim_depth), (0, 0))).astype(jnp.float32)
    back = depthwise(wide_grad, dw_kernel[::-1, ::-1], height, breadth)
    image_grad = (upstream.reshape(height, breadth, channels) + back).astype(jnp.bfloat16)
    kernel_local = kernel_terms(wide_image, mixed_grad.astype(jnp.float32), kernel_size)
    flat = sum_rows(jnp.concatenate([kernel_local.reshape(-1), scale_term]))
    kernel_grad = flat[: kernel_local.size].reshape(kernel_local.shape)
    scale_grad = flat[kernel_local.size :]
    return (result, image_grad, expand_grad, project_grad, kernel_grad, scale_grad)


def solution(mesh):
    tensor_size, rows_size = mesh.devices.shape
    far = 2
    core = 2
    near = 2
    fine = Mesh(
        mesh.devices.reshape(far, tensor_size // (far * core), core, near, rows_size // near),
        ("xh", "z", "c", "xl", "y"),
    )
    return jax.shard_map(
        per_device,
        mesh=fine,
        in_specs=(
            P(ROWS, None, TENSOR),
            P(None, None, TENSOR),
            P(TENSOR),
            P(),
            P(),
            P(ROWS, TENSOR),
            P(TENSOR),
            P(TENSOR, ROWS),
            P(TENSOR),
            P(TENSOR),
            P(ROWS, None, TENSOR),
        ),
        out_specs=(
            P(ROWS, None, TENSOR),
            P(ROWS, None, TENSOR),
            P(ROWS, TENSOR),
            P(TENSOR, ROWS),
            P(None, None, TENSOR),
            P(TENSOR),
        ),
        check_vma=False,
    )
```

```python
import math

import jax
import jax.numpy as jnp
from jax import lax
from jax.sharding import Mesh
from jax.sharding import PartitionSpec as P

EPSILON = 1e-06

TENSOR = ("xh", "z", "c")
ROWS = ("xl", "y")


def shifted(x, axis, count, step):
    return lax.ppermute(x, axis, [(i, (i + step) % count) for i in range(count)])


def order2(mine, other, index):
    first = jnp.where(index == 0, mine, other)
    second = jnp.where(index == 0, other, mine)
    return jnp.stack([first, second])


def ring_gather(x, axis, count, out_axis=0):
    me = lax.axis_index(axis)
    ahead = count // 2
    behind = count - 1 - ahead
    rel = {0: x}
    fwd = x
    for s in range(1, ahead + 1):
        fwd = shifted(fwd, axis, count, 1)
        rel[-s] = fwd
    bwd = x
    for s in range(1, behind + 1):
        bwd = shifted(bwd, axis, count, -1)
        rel[s] = bwd
    placed = jnp.zeros(x.shape[:out_axis] + (count,) + x.shape[out_axis:], x.dtype)
    for k, part in rel.items():
        placed = lax.dynamic_update_index_in_dim(placed, part, (me + k + count) % count, out_axis)
    return placed


def ring_scatter(blocks, axis, count, send_dtype):
    me = lax.axis_index(axis)

    def block(k):
        return lax.dynamic_index_in_dim(blocks, (me + k + count) % count, axis=0, keepdims=False).astype(
            jnp.float32
        )

    ahead = count // 2
    behind = count - 1 - ahead
    total = block(0)
    acc = None
    for s in range(1, ahead + 1):
        part = block(ahead + 1 - s)
        part = part if acc is None else acc + part
        acc = shifted(part.astype(send_dtype), axis, count, 1).astype(jnp.float32)
    total = total + acc
    acc = None
    for s in range(1, behind + 1):
        part = block(-(behind + 1 - s))
        part = part if acc is None else acc + part
        acc = shifted(part.astype(send_dtype), axis, count, -1).astype(jnp.float32)
    if acc is not None:
        total = total + acc
    return total


def gather_channels(x):
    core = lax.axis_index("c")
    far = lax.axis_index("xh")
    kinds, positions, width = x.shape
    half = positions // 2
    own = lax.dynamic_slice_in_dim(x, core * half, half, axis=1)
    sent = lax.dynamic_slice_in_dim(x, (1 - core) * half, half, axis=1)
    got = shifted(sent, "c", 2, 1)
    chip = jnp.concatenate(
        [jnp.where(core == 0, own, got), jnp.where(core == 0, got, own)], axis=2
    )
    other = shifted(chip, "xh", 2, 1)
    pair = jnp.stack(
        [jnp.where(far == 0, chip, other), jnp.where(far == 0, other, chip)], axis=2
    )
    ring = ring_gather(pair, "z", lax.axis_size("z"), 3)
    return ring.reshape(kinds, half, -1)


def scatter_channels(chip, extra):
    core = lax.axis_index("c")
    far = lax.axis_index("xh")
    zs = lax.axis_size("z")
    half, features = chip.shape
    width = features // (4 * zs)
    spread = jnp.broadcast_to(
        extra.astype(jnp.float32)[:, None, None, None, :], (half, 2, zs, 2, extra.shape[1])
    )
    chip = jnp.concatenate([chip.astype(jnp.float32).reshape(half, 2, zs, 2, width), spread], axis=4)
    blocks = jnp.transpose(chip, (2, 0, 1, 3, 4))
    ring = ring_scatter(blocks, "z", zs, jnp.bfloat16)
    mine = lax.dynamic_index_in_dim(ring, far, axis=1, keepdims=False)
    theirs = lax.dynamic_index_in_dim(ring, 1 - far, axis=1, keepdims=False)
    pair = mine + shifted(theirs.astype(jnp.bfloat16), "xh", 2, 1).astype(jnp.float32)
    keep = lax.dynamic_index_in_dim(pair, core, axis=1, keepdims=False)
    give = lax.dynamic_index_in_dim(pair, 1 - core, axis=1, keepdims=False)
    both = by_core(keep, shifted(give, "c", 2, 1), 0)
    return both[:, :width], both[:, width:]


def by_core(mine, other, axis):
    core = lax.axis_index("c")
    return jnp.concatenate(
        [jnp.where(core == 0, mine, other), jnp.where(core == 0, other, mine)], axis=axis
    )


def chip_blocks(x, axis):
    return by_core(x, shifted(x, "c", 2, 1), axis)


def fold_cores(term, axis):
    core = lax.axis_index("c")
    size = term.shape[axis] // 2
    mine = lax.dynamic_slice_in_dim(term, core * size, size, axis=axis)
    give = lax.dynamic_slice_in_dim(term, (1 - core) * size, size, axis=axis)
    return mine + shifted(give.astype(jnp.bfloat16), "c", 2, 1).astype(jnp.float32)


def gather_rows(w, dim):
    return lax.all_gather(w, ROWS, axis=dim, tiled=True)


def scatter_rows(term, dim):
    return lax.psum_scatter(
        term.astype(jnp.bfloat16), ROWS, scatter_dimension=dim, tiled=True
    ).astype(jnp.float32)


def sum_rows(v):
    v = v + shifted(v, "xl", 2, 1)
    return jnp.sum(ring_gather(v, "y", lax.axis_size("y")), axis=0)


def extended(cells, width):
    count = lax.axis_size(ROWS)
    ends = count - 1
    head = lax.slice_in_dim(cells, 0, width, axis=0)
    tail = lax.slice_in_dim(cells, cells.shape[0] - width, cells.shape[0], axis=0)
    return jnp.concatenate(
        [
            lax.ppermute(tail, ROWS, [(i, (i + 1) % count) for i in range(ends)]),
            cells,
            lax.ppermute(head, ROWS, [((i + 1) % count, i) for i in range(ends)]),
        ],
        axis=0,
    )


def gelu_exact(values):
    return 0.5 * values * (1.0 + lax.erf(values * (1.0 / math.sqrt(2.0))))


def gelu_slope(values):
    cumulative = 0.5 * (1.0 + lax.erf(values * (1.0 / math.sqrt(2.0))))
    density = jnp.exp(-0.5 * values * values) * (1.0 / math.sqrt(2.0 * math.pi))
    return cumulative + values * density


def depthwise(padded, kernel, height, breadth):
    kernel_size = kernel.shape[0]
    summed = jnp.zeros((height, breadth, kernel.shape[2]), jnp.float32)
    for row_shift in range(kernel_size):
        for col_shift in range(kernel_size):
            window = padded[row_shift : row_shift + height, col_shift : col_shift + breadth]
            summed = summed + kernel[row_shift, col_shift].astype(jnp.float32) * window
    return summed


def kernel_terms(padded, gradient, kernel_size):
    height, breadth = (gradient.shape[0], gradient.shape[1])
    kernel_rows = []
    for row_shift in range(kernel_size):
        kernel_line = []
        for col_shift in range(kernel_size):
            window = padded[row_shift : row_shift + height, col_shift : col_shift + breadth]
            kernel_line.append(jnp.sum(window * gradient, axis=(0, 1)))
        kernel_rows.append(jnp.stack(kernel_line))
    return jnp.stack(kernel_rows)


def contract_last(left, right):
    return lax.dot_general(
        left, right, (((1,), (1,)), ((), ())), preferred_element_type=jnp.float32
    )


def contract_first(left, right):
    return lax.dot_general(
        left, right, (((0,), (0,)), ((), ())), preferred_element_type=jnp.float32
    )


def per_device(
    image,
    dw_kernel,
    dw_bias,
    norm_gain,
    norm_bias,
    w_expand,
    b_expand,
    w_project,
    b_project,
    layer_scale,
    out_grad,
):
    kernel_size = dw_kernel.shape[0]
    rim_depth = kernel_size // 2
    height, breadth, channels = image.shape
    positions = height * breadth
    features = norm_gain.shape[0]
    channel_start = lax.axis_index(TENSOR) * channels

    core = lax.axis_index("c")
    half = positions // 2
    hidden_width = w_expand.shape[1]
    w_expand_chip = chip_blocks(gather_rows(w_expand, 0), 1)
    w_project_chip = chip_blocks(gather_rows(w_project, 1), 0)
    b_expand_chip = chip_blocks(b_expand, 0)
    upstream = out_grad.reshape(positions, channels).astype(jnp.float32)
    scaled_grad = (upstream * layer_scale).astype(jnp.bfloat16)

    rimmed = extended(image, rim_depth)
    wide_image = jnp.pad(rimmed, ((0, 0), (rim_depth, rim_depth), (0, 0))).astype(jnp.float32)
    convolved = depthwise(wide_image, dw_kernel, height, breadth) + dw_bias
    mixed = convolved.astype(jnp.bfloat16).reshape(positions, channels)
    gathered = gather_channels(jnp.stack([mixed, scaled_grad]))
    all_mixed = gathered[0].astype(jnp.float32)
    grad_panels = gathered[1]
    average = jnp.sum(all_mixed, 1, keepdims=True) / features
    mean_square = jnp.sum(all_mixed * all_mixed, 1, keepdims=True) / features
    inv_std = lax.rsqrt(mean_square - average * average + EPSILON)
    centred = (all_mixed - average) * inv_std
    normed = (centred * norm_gain + norm_bias).astype(jnp.bfloat16)
    pre = jnp.dot(normed, w_expand_chip, preferred_element_type=jnp.float32) + b_expand_chip
    hidden = gelu_exact(pre).astype(jnp.bfloat16)
    hidden_grad = contract_last(grad_panels, w_project_chip)
    pre_grad = (hidden_grad * gelu_slope(pre)).astype(jnp.bfloat16)
    normed_partial = sum(
        contract_last(
            pre_grad[:, g * hidden_width : (g + 1) * hidden_width],
            w_expand_chip[:, g * hidden_width : (g + 1) * hidden_width],
        )
        .astype(jnp.bfloat16)
        .astype(jnp.float32)
        for g in range(2)
    )
    gain_partial = normed_partial * norm_gain
    stat_partial = jnp.stack([jnp.sum(gain_partial, 1), jnp.sum(gain_partial * centred, 1)], axis=1)
    late_hidden, normed_partial, stat_partial = lax.optimization_barrier(
        (hidden, normed_partial, stat_partial)
    )
    normed_grad, stats = scatter_channels(normed_partial, stat_partial)
    stats = stats.T
    project_term = fold_cores(contract_first(grad_panels, hidden), 1)
    project_grad = scatter_rows(project_term, 0).T
    expand_term = fold_cores(contract_first(normed, pre_grad), 1)
    late_hidden, expand_term = lax.optimization_barrier((late_hidden, expand_term))
    expand_grad = scatter_rows(expand_term, 0)

    partial_out = sum(
        jnp.dot(
            late_hidden[:, g * hidden_width : (g + 1) * hidden_width],
            w_project_chip[g * hidden_width : (g + 1) * hidden_width],
            preferred_element_type=jnp.float32,
        )
        .astype(jnp.bfloat16)
        .astype(jnp.float32)
        for g in range(2)
    )
    projected, _ = scatter_channels(partial_out, jnp.zeros((half, 0)))
    projected = projected + b_project
    residual = image.reshape(positions, channels).astype(jnp.float32)
    result = (
        (residual + layer_scale * projected).astype(jnp.bfloat16).reshape(height, breadth, channels)
    )
    scale_term = jnp.sum(upstream * projected, 0)

    row_stats = chip_blocks(jnp.concatenate([average, inv_std], axis=1), 0)
    gain_part = lax.dynamic_slice_in_dim(norm_gain, channel_start, channels)
    centred_part = (mixed.astype(jnp.float32) - row_stats[:, :1]) * row_stats[:, 1:]
    part_std = row_stats[:, 1:]
    gain_grad = normed_grad * gain_part
    plain_mean = stats[0][:, None] / features
    centred_mean = stats[1][:, None] / features
    mixed_grad = (part_std * (gain_grad - plain_mean - centred_part * centred_mean)).astype(
        jnp.bfloat16
    )
    mixed_grad = mixed_grad.reshape(height, breadth, channels)
    grad_rimmed = extended(mixed_grad, rim_depth)
    wide_grad = jnp.pad(grad_rimmed, ((0, 0), (rim_depth, rim_depth), (0, 0))).astype(jnp.float32)
    back = depthwise(wide_grad, dw_kernel[::-1, ::-1], height, breadth)
    image_grad = (upstream.reshape(height, breadth, channels) + back).astype(jnp.bfloat16)
    kernel_local = kernel_terms(wide_image, mixed_grad.astype(jnp.float32), kernel_size)
    flat = sum_rows(jnp.concatenate([kernel_local.reshape(-1), scale_term]))
    kernel_grad = flat[: kernel_local.size].reshape(kernel_local.shape)
    scale_grad = flat[kernel_local.size :]
    return (result, image_grad, expand_grad, project_grad, kernel_grad, scale_grad)


def solution(mesh):
    tensor_size, rows_size = mesh.devices.shape
    far = 2
    core = 2
    near = 2
    fine = Mesh(
        mesh.devices.reshape(far, tensor_size // (far * core), core, near, rows_size // near),
        ("xh", "z", "c", "xl", "y"),
    )
    return jax.shard_map(
        per_device,
        mesh=fine,
        in_specs=(
            P(ROWS, None, TENSOR),
            P(None, None, TENSOR),
            P(TENSOR),
            P(),
            P(),
            P(ROWS, TENSOR),
            P(TENSOR),
            P(TENSOR, ROWS),
            P(TENSOR),
            P(TENSOR),
            P(ROWS, None, TENSOR),
        ),
        out_specs=(
            P(ROWS, None, TENSOR),
            P(ROWS, None, TENSOR),
            P(ROWS, TENSOR),
            P(TENSOR, ROWS),
            P(None, None, TENSOR),
            P(TENSOR),
        ),
        check_vma=False,
    )
```

```python
import math

import jax
import jax.numpy as jnp
from jax import lax
from jax.sharding import Mesh
from jax.sharding import PartitionSpec as P

EPSILON = 1e-06

TENSOR = ("xh", "z", "c")
ROWS = ("xl", "y")


def shifted(x, axis, count, step):
    return lax.ppermute(x, axis, [(i, (i + step) % count) for i in range(count)])


def order2(mine, other, index):
    first = jnp.where(index == 0, mine, other)
    second = jnp.where(index == 0, other, mine)
    return jnp.stack([first, second])


def ring_gather(x, axis, count, out_axis=0):
    me = lax.axis_index(axis)
    ahead = count // 2
    behind = count - 1 - ahead
    rel = {0: x}
    fwd = x
    for s in range(1, ahead + 1):
        fwd = shifted(fwd, axis, count, 1)
        rel[-s] = fwd
    bwd = x
    for s in range(1, behind + 1):
        bwd = shifted(bwd, axis, count, -1)
        rel[s] = bwd
    placed = jnp.zeros(x.shape[:out_axis] + (count,) + x.shape[out_axis:], x.dtype)
    for k, part in rel.items():
        placed = lax.dynamic_update_index_in_dim(placed, part, (me + k + count) % count, out_axis)
    return placed


def ring_scatter(blocks, axis, count, send_dtype):
    me = lax.axis_index(axis)

    def block(k):
        return lax.dynamic_index_in_dim(blocks, (me + k + count) % count, axis=0, keepdims=False).astype(
            jnp.float32
        )

    ahead = count // 2
    behind = count - 1 - ahead
    total = block(0)
    acc = None
    for s in range(1, ahead + 1):
        part = block(ahead + 1 - s)
        part = part if acc is None else acc + part
        acc = shifted(part.astype(send_dtype), axis, count, 1).astype(jnp.float32)
    total = total + acc
    acc = None
    for s in range(1, behind + 1):
        part = block(-(behind + 1 - s))
        part = part if acc is None else acc + part
        acc = shifted(part.astype(send_dtype), axis, count, -1).astype(jnp.float32)
    if acc is not None:
        total = total + acc
    return total


def gather_channels(x):
    core = lax.axis_index("c")
    far = lax.axis_index("xh")
    kinds, positions, width = x.shape
    half = positions // 2
    own = lax.dynamic_slice_in_dim(x, core * half, half, axis=1)
    sent = lax.dynamic_slice_in_dim(x, (1 - core) * half, half, axis=1)
    got = shifted(sent, "c", 2, 1)
    chip = jnp.concatenate(
        [jnp.where(core == 0, own, got), jnp.where(core == 0, got, own)], axis=2
    )
    other = shifted(chip, "xh", 2, 1)
    pair = jnp.stack(
        [jnp.where(far == 0, chip, other), jnp.where(far == 0, other, chip)], axis=2
    )
    ring = ring_gather(pair, "z", lax.axis_size("z"), 3)
    return ring.reshape(kinds, half, -1)


def scatter_channels(chip, extra):
    core = lax.axis_index("c")
    far = lax.axis_index("xh")
    zs = lax.axis_size("z")
    half, features = chip.shape
    width = features // (4 * zs)
    spread = jnp.broadcast_to(
        extra.astype(jnp.float32)[:, None, None, None, :], (half, 2, zs, 2, extra.shape[1])
    )
    chip = jnp.concatenate([chip.astype(jnp.float32).reshape(half, 2, zs, 2, width), spread], axis=4)
    blocks = jnp.transpose(chip, (2, 0, 1, 3, 4))
    ring = ring_scatter(blocks, "z", zs, jnp.bfloat16)
    mine = lax.dynamic_index_in_dim(ring, far, axis=1, keepdims=False)
    theirs = lax.dynamic_index_in_dim(ring, 1 - far, axis=1, keepdims=False)
    pair = mine + shifted(theirs.astype(jnp.bfloat16), "xh", 2, 1).astype(jnp.float32)
    keep = lax.dynamic_index_in_dim(pair, core, axis=1, keepdims=False)
    give = lax.dynamic_index_in_dim(pair, 1 - core, axis=1, keepdims=False)
    both = by_core(keep, shifted(give, "c", 2, 1), 0)
    return both[:, :width], both[:, width:]


def by_core(mine, other, axis):
    core = lax.axis_index("c")
    return jnp.concatenate(
        [jnp.where(core == 0, mine, other), jnp.where(core == 0, other, mine)], axis=axis
    )


def chip_blocks(x, axis):
    return by_core(x, shifted(x, "c", 2, 1), axis)


def fold_cores(term, axis):
    core = lax.axis_index("c")
    size = term.shape[axis] // 2
    mine = lax.dynamic_slice_in_dim(term, core * size, size, axis=axis)
    give = lax.dynamic_slice_in_dim(term, (1 - core) * size, size, axis=axis)
    return mine + shifted(give.astype(jnp.bfloat16), "c", 2, 1).astype(jnp.float32)


def gather_rows(w, dim):
    return lax.all_gather(w, ROWS, axis=dim, tiled=True)


def scatter_rows(term, dim):
    return lax.psum_scatter(
        term.astype(jnp.bfloat16), ROWS, scatter_dimension=dim, tiled=True
    ).astype(jnp.float32)


def sum_rows(v):
    v = v + shifted(v, "xl", 2, 1)
    return jnp.sum(ring_gather(v, "y", lax.axis_size("y")), axis=0)


def extended(cells, width):
    count = lax.axis_size(ROWS)
    ends = count - 1
    head = lax.slice_in_dim(cells, 0, width, axis=0)
    tail = lax.slice_in_dim(cells, cells.shape[0] - width, cells.shape[0], axis=0)
    return jnp.concatenate(
        [
            lax.ppermute(tail, ROWS, [(i, (i + 1) % count) for i in range(ends)]),
            cells,
            lax.ppermute(head, ROWS, [((i + 1) % count, i) for i in range(ends)]),
        ],
        axis=0,
    )


def gelu_exact(values):
    return 0.5 * values * (1.0 + lax.erf(values * (1.0 / math.sqrt(2.0))))


def gelu_slope(values):
    cumulative = 0.5 * (1.0 + lax.erf(values * (1.0 / math.sqrt(2.0))))
    density = jnp.exp(-0.5 * values * values) * (1.0 / math.sqrt(2.0 * math.pi))
    return cumulative + values * density


def depthwise(padded, kernel, height, breadth):
    kernel_size = kernel.shape[0]
    summed = jnp.zeros((height, breadth, kernel.shape[2]), jnp.float32)
    for row_shift in range(kernel_size):
        for col_shift in range(kernel_size):
            window = padded[row_shift : row_shift + height, col_shift : col_shift + breadth]
            summed = summed + kernel[row_shift, col_shift].astype(jnp.float32) * window
    return summed


def kernel_terms(padded, gradient, kernel_size):
    height, breadth = (gradient.shape[0], gradient.shape[1])
    kernel_rows = []
    for row_shift in range(kernel_size):
        kernel_line = []
        for col_shift in range(kernel_size):
            window = padded[row_shift : row_shift + height, col_shift : col_shift + breadth]
            kernel_line.append(jnp.sum(window * gradient, axis=(0, 1)))
        kernel_rows.append(jnp.stack(kernel_line))
    return jnp.stack(kernel_rows)


def contract_last(left, right):
    return lax.dot_general(
        left, right, (((1,), (1,)), ((), ())), preferred_element_type=jnp.float32
    )


def contract_first(left, right):
    return lax.dot_general(
        left, right, (((0,), (0,)), ((), ())), preferred_element_type=jnp.float32
    )


def per_device(
    image,
    dw_kernel,
    dw_bias,
    norm_gain,
    norm_bias,
    w_expand,
    b_expand,
    w_project,
    b_project,
    layer_scale,
    out_grad,
):
    kernel_size = dw_kernel.shape[0]
    rim_depth = kernel_size // 2
    height, breadth, channels = image.shape
    positions = height * breadth
    features = norm_gain.shape[0]
    channel_start = lax.axis_index(TENSOR) * channels

    core = lax.axis_index("c")
    half = positions // 2
    hidden_width = w_expand.shape[1]
    w_expand_chip = chip_blocks(gather_rows(w_expand, 0), 1)
    w_project_chip = chip_blocks(gather_rows(w_project, 1), 0)
    b_expand_chip = chip_blocks(b_expand, 0)
    upstream = out_grad.reshape(positions, channels).astype(jnp.float32)
    scaled_grad = (upstream * layer_scale).astype(jnp.bfloat16)

    rimmed = extended(image, rim_depth)
    wide_image = jnp.pad(rimmed, ((0, 0), (rim_depth, rim_depth), (0, 0))).astype(jnp.float32)
    convolved = depthwise(wide_image, dw_kernel, height, breadth) + dw_bias
    mixed = convolved.astype(jnp.bfloat16).reshape(positions, channels)
    gathered_mixed = gather_channels(mixed[None])[0]
    gathered_mixed, scaled_grad = lax.optimization_barrier((gathered_mixed, scaled_grad))
    grad_panels = gather_channels(scaled_grad[None])[0]
    all_mixed = gathered_mixed.astype(jnp.float32)
    average = jnp.sum(all_mixed, 1, keepdims=True) / features
    mean_square = jnp.sum(all_mixed * all_mixed, 1, keepdims=True) / features
    inv_std = lax.rsqrt(mean_square - average * average + EPSILON)
    centred = (all_mixed - average) * inv_std
    normed = (centred * norm_gain + norm_bias).astype(jnp.bfloat16)
    pre = jnp.dot(normed, w_expand_chip, preferred_element_type=jnp.float32) + b_expand_chip
    hidden = gelu_exact(pre).astype(jnp.bfloat16)
    hidden_grad = contract_last(grad_panels, w_project_chip)
    pre_grad = (hidden_grad * gelu_slope(pre)).astype(jnp.bfloat16)
    normed_partial = sum(
        contract_last(
            pre_grad[:, g * hidden_width : (g + 1) * hidden_width],
            w_expand_chip[:, g * hidden_width : (g + 1) * hidden_width],
        )
        .astype(jnp.bfloat16)
        .astype(jnp.float32)
        for g in range(2)
    )
    gain_partial = normed_partial * norm_gain
    stat_partial = jnp.stack([jnp.sum(gain_partial, 1), jnp.sum(gain_partial * centred, 1)], axis=1)
    late_hidden, normed_partial, stat_partial = lax.optimization_barrier(
        (hidden, normed_partial, stat_partial)
    )
    normed_grad, stats = scatter_channels(normed_partial, stat_partial)
    stats = stats.T
    expand_grad = scatter_rows(fold_cores(contract_first(normed, pre_grad), 1), 0)
    project_term = fold_cores(contract_first(hidden, grad_panels), 0)
    project_grad = scatter_rows(project_term, 1)

    partial_out = sum(
        jnp.dot(
            late_hidden[:, g * hidden_width : (g + 1) * hidden_width],
            w_project_chip[g * hidden_width : (g + 1) * hidden_width],
            preferred_element_type=jnp.float32,
        )
        .astype(jnp.bfloat16)
        .astype(jnp.float32)
        for g in range(2)
    )
    projected, _ = scatter_channels(partial_out, jnp.zeros((half, 0)))
    projected = projected + b_project
    residual = image.reshape(positions, channels).astype(jnp.float32)
    result = (
        (residual + layer_scale * projected).astype(jnp.bfloat16).reshape(height, breadth, channels)
    )
    scale_term = jnp.sum(upstream * projected, 0)

    row_stats = chip_blocks(jnp.concatenate([average, inv_std], axis=1), 0)
    gain_part = lax.dynamic_slice_in_dim(norm_gain, channel_start, channels)
    centred_part = (mixed.astype(jnp.float32) - row_stats[:, :1]) * row_stats[:, 1:]
    part_std = row_stats[:, 1:]
    gain_grad = normed_grad * gain_part
    plain_mean = stats[0][:, None] / features
    centred_mean = stats[1][:, None] / features
    mixed_grad = (part_std * (gain_grad - plain_mean - centred_part * centred_mean)).astype(
        jnp.bfloat16
    )
    mixed_grad = mixed_grad.reshape(height, breadth, channels)
    grad_rimmed = extended(mixed_grad, rim_depth)
    wide_grad = jnp.pad(grad_rimmed, ((0, 0), (rim_depth, rim_depth), (0, 0))).astype(jnp.float32)
    back = depthwise(wide_grad, dw_kernel[::-1, ::-1], height, breadth)
    image_grad = (upstream.reshape(height, breadth, channels) + back).astype(jnp.bfloat16)
    kernel_local = kernel_terms(wide_image, mixed_grad.astype(jnp.float32), kernel_size)
    flat = sum_rows(jnp.concatenate([kernel_local.reshape(-1), scale_term]))
    kernel_grad = flat[: kernel_local.size].reshape(kernel_local.shape)
    scale_grad = flat[kernel_local.size :]
    return (result, image_grad, expand_grad, project_grad, kernel_grad, scale_grad)


def solution(mesh):
    tensor_size, rows_size = mesh.devices.shape
    far = 2
    core = 2
    near = 2
    fine = Mesh(
        mesh.devices.reshape(far, tensor_size // (far * core), core, near, rows_size // near),
        ("xh", "z", "c", "xl", "y"),
    )
    return jax.shard_map(
        per_device,
        mesh=fine,
        in_specs=(
            P(ROWS, None, TENSOR),
            P(None, None, TENSOR),
            P(TENSOR),
            P(),
            P(),
            P(ROWS, TENSOR),
            P(TENSOR),
            P(TENSOR, ROWS),
            P(TENSOR),
            P(TENSOR),
            P(ROWS, None, TENSOR),
        ),
        out_specs=(
            P(ROWS, None, TENSOR),
            P(ROWS, None, TENSOR),
            P(ROWS, TENSOR),
            P(TENSOR, ROWS),
            P(None, None, TENSOR),
            P(TENSOR),
        ),
        check_vma=False,
    )
```

```python
import math

import jax
import jax.numpy as jnp
from jax import lax
from jax.sharding import Mesh
from jax.sharding import PartitionSpec as P

EPSILON = 1e-06

TENSOR = ("xh", "z", "c")
ROWS = ("xl", "y")


def shifted(x, axis, count, step):
    return lax.ppermute(x, axis, [(i, (i + step) % count) for i in range(count)])


def order2(mine, other, index):
    first = jnp.where(index == 0, mine, other)
    second = jnp.where(index == 0, other, mine)
    return jnp.stack([first, second])


def ring_gather(x, axis, count, out_axis=0):
    me = lax.axis_index(axis)
    ahead = count // 2
    behind = count - 1 - ahead
    rel = {0: x}
    fwd = x
    for s in range(1, ahead + 1):
        fwd = shifted(fwd, axis, count, 1)
        rel[-s] = fwd
    bwd = x
    for s in range(1, behind + 1):
        bwd = shifted(bwd, axis, count, -1)
        rel[s] = bwd
    placed = jnp.zeros(x.shape[:out_axis] + (count,) + x.shape[out_axis:], x.dtype)
    for k, part in rel.items():
        placed = lax.dynamic_update_index_in_dim(placed, part, (me + k + count) % count, out_axis)
    return placed


def ring_scatter(blocks, axis, count, send_dtype):
    me = lax.axis_index(axis)

    def block(k):
        return lax.dynamic_index_in_dim(blocks, (me + k + count) % count, axis=0, keepdims=False).astype(
            jnp.float32
        )

    ahead = count // 2
    behind = count - 1 - ahead
    total = block(0)
    acc = None
    for s in range(1, ahead + 1):
        part = block(ahead + 1 - s)
        part = part if acc is None else acc + part
        acc = shifted(part.astype(send_dtype), axis, count, 1).astype(jnp.float32)
    total = total + acc
    acc = None
    for s in range(1, behind + 1):
        part = block(-(behind + 1 - s))
        part = part if acc is None else acc + part
        acc = shifted(part.astype(send_dtype), axis, count, -1).astype(jnp.float32)
    if acc is not None:
        total = total + acc
    return total


def gather_channels(x):
    core = lax.axis_index("c")
    far = lax.axis_index("xh")
    kinds, positions, width = x.shape
    half = positions // 2
    own = lax.dynamic_slice_in_dim(x, core * half, half, axis=1)
    sent = lax.dynamic_slice_in_dim(x, (1 - core) * half, half, axis=1)
    got = shifted(sent, "c", 2, 1)
    chip = jnp.concatenate(
        [jnp.where(core == 0, own, got), jnp.where(core == 0, got, own)], axis=2
    )
    other = shifted(chip, "xh", 2, 1)
    pair = jnp.stack(
        [jnp.where(far == 0, chip, other), jnp.where(far == 0, other, chip)], axis=2
    )
    ring = ring_gather(pair, "z", lax.axis_size("z"), 3)
    return ring.reshape(kinds, half, -1)


def scatter_channels(chip, extra):
    core = lax.axis_index("c")
    far = lax.axis_index("xh")
    zs = lax.axis_size("z")
    half, features = chip.shape
    width = features // (4 * zs)
    spread = jnp.broadcast_to(
        extra.astype(jnp.float32)[:, None, None, None, :], (half, 2, zs, 2, extra.shape[1])
    )
    chip = jnp.concatenate([chip.astype(jnp.float32).reshape(half, 2, zs, 2, width), spread], axis=4)
    blocks = jnp.transpose(chip, (2, 0, 1, 3, 4))
    ring = ring_scatter(blocks, "z", zs, jnp.bfloat16)
    mine = lax.dynamic_index_in_dim(ring, far, axis=1, keepdims=False)
    theirs = lax.dynamic_index_in_dim(ring, 1 - far, axis=1, keepdims=False)
    pair = mine + shifted(theirs.astype(jnp.bfloat16), "xh", 2, 1).astype(jnp.float32)
    keep = lax.dynamic_index_in_dim(pair, core, axis=1, keepdims=False)
    give = lax.dynamic_index_in_dim(pair, 1 - core, axis=1, keepdims=False)
    both = by_core(keep, shifted(give, "c", 2, 1), 0)
    return both[:, :width], both[:, width:]


def by_core(mine, other, axis):
    core = lax.axis_index("c")
    return jnp.concatenate(
        [jnp.where(core == 0, mine, other), jnp.where(core == 0, other, mine)], axis=axis
    )


def chip_blocks(x, axis):
    return by_core(x, shifted(x, "c", 2, 1), axis)


def fold_cores(term, axis):
    core = lax.axis_index("c")
    size = term.shape[axis] // 2
    mine = lax.dynamic_slice_in_dim(term, core * size, size, axis=axis)
    give = lax.dynamic_slice_in_dim(term, (1 - core) * size, size, axis=axis)
    return mine + shifted(give.astype(jnp.bfloat16), "c", 2, 1).astype(jnp.float32)


def gather_rows(w, dim):
    return lax.all_gather(w, ROWS, axis=dim, tiled=True)


def scatter_rows(term, dim):
    return lax.psum_scatter(
        term.astype(jnp.bfloat16), ROWS, scatter_dimension=dim, tiled=True
    ).astype(jnp.float32)


def scatter_chip_rows(blocks):
    flat = blocks.reshape((-1,) + blocks.shape[3:]).astype(jnp.bfloat16)
    return lax.psum_scatter(
        flat, ("c",) + ROWS, scatter_dimension=0, tiled=True
    ).astype(jnp.float32)


def sum_rows(v):
    v = v + shifted(v, "xl", 2, 1)
    return jnp.sum(ring_gather(v, "y", lax.axis_size("y")), axis=0)


def extended(cells, width):
    count = lax.axis_size(ROWS)
    ends = count - 1
    head = lax.slice_in_dim(cells, 0, width, axis=0)
    tail = lax.slice_in_dim(cells, cells.shape[0] - width, cells.shape[0], axis=0)
    return jnp.concatenate(
        [
            lax.ppermute(tail, ROWS, [(i, (i + 1) % count) for i in range(ends)]),
            cells,
            lax.ppermute(head, ROWS, [((i + 1) % count, i) for i in range(ends)]),
        ],
        axis=0,
    )


def gelu_exact(values):
    return 0.5 * values * (1.0 + lax.erf(values * (1.0 / math.sqrt(2.0))))


def gelu_slope(values):
    cumulative = 0.5 * (1.0 + lax.erf(values * (1.0 / math.sqrt(2.0))))
    density = jnp.exp(-0.5 * values * values) * (1.0 / math.sqrt(2.0 * math.pi))
    return cumulative + values * density


def depthwise(padded, kernel, height, breadth):
    kernel_size = kernel.shape[0]
    summed = jnp.zeros((height, breadth, kernel.shape[2]), jnp.float32)
    for row_shift in range(kernel_size):
        for col_shift in range(kernel_size):
            window = padded[row_shift : row_shift + height, col_shift : col_shift + breadth]
            summed = summed + kernel[row_shift, col_shift].astype(jnp.float32) * window
    return summed


def kernel_terms(padded, gradient, kernel_size):
    height, breadth = (gradient.shape[0], gradient.shape[1])
    kernel_rows = []
    for row_shift in range(kernel_size):
        kernel_line = []
        for col_shift in range(kernel_size):
            window = padded[row_shift : row_shift + height, col_shift : col_shift + breadth]
            kernel_line.append(jnp.sum(window * gradient, axis=(0, 1)))
        kernel_rows.append(jnp.stack(kernel_line))
    return jnp.stack(kernel_rows)


def contract_last(left, right):
    return lax.dot_general(
        left, right, (((1,), (1,)), ((), ())), preferred_element_type=jnp.float32
    )


def contract_first(left, right):
    return lax.dot_general(
        left, right, (((0,), (0,)), ((), ())), preferred_element_type=jnp.float32
    )


def per_device(
    image,
    dw_kernel,
    dw_bias,
    norm_gain,
    norm_bias,
    w_expand,
    b_expand,
    w_project,
    b_project,
    layer_scale,
    out_grad,
):
    kernel_size = dw_kernel.shape[0]
    rim_depth = kernel_size // 2
    height, breadth, channels = image.shape
    positions = height * breadth
    features = norm_gain.shape[0]
    channel_start = lax.axis_index(TENSOR) * channels

    core = lax.axis_index("c")
    half = positions // 2
    hidden_width = w_expand.shape[1]
    ys = lax.axis_size("y")
    w_expand_chip = chip_blocks(gather_rows(w_expand, 0), 1)
    w_project_chip = chip_blocks(gather_rows(w_project, 1), 0)
    b_expand_chip = chip_blocks(b_expand, 0)
    upstream = out_grad.reshape(positions, channels).astype(jnp.float32)
    scaled_grad = (upstream * layer_scale).astype(jnp.bfloat16)

    rimmed = extended(image, rim_depth)
    wide_image = jnp.pad(rimmed, ((0, 0), (rim_depth, rim_depth), (0, 0))).astype(jnp.float32)
    convolved = depthwise(wide_image, dw_kernel, height, breadth) + dw_bias
    mixed = convolved.astype(jnp.bfloat16).reshape(positions, channels)
    gathered = gather_channels(jnp.stack([mixed, scaled_grad]))
    all_mixed = gathered[0].astype(jnp.float32)
    grad_panels = gathered[1]
    average = jnp.sum(all_mixed, 1, keepdims=True) / features
    mean_square = jnp.sum(all_mixed * all_mixed, 1, keepdims=True) / features
    inv_std = lax.rsqrt(mean_square - average * average + EPSILON)
    centred = (all_mixed - average) * inv_std
    normed = (centred * norm_gain + norm_bias).astype(jnp.bfloat16)
    pre = jnp.dot(normed, w_expand_chip, preferred_element_type=jnp.float32) + b_expand_chip
    hidden = gelu_exact(pre).astype(jnp.bfloat16)
    hidden_grad = contract_last(grad_panels, w_project_chip)
    pre_grad = (hidden_grad * gelu_slope(pre)).astype(jnp.bfloat16)
    normed_partial = sum(
        contract_last(
            pre_grad[:, g * hidden_width : (g + 1) * hidden_width],
            w_expand_chip[:, g * hidden_width : (g + 1) * hidden_width],
        )
        .astype(jnp.bfloat16)
        .astype(jnp.float32)
        for g in range(2)
    )
    gain_partial = normed_partial * norm_gain
    stat_partial = jnp.stack([jnp.sum(gain_partial, 1), jnp.sum(gain_partial * centred, 1)], axis=1)
    late_hidden, normed_partial, stat_partial = lax.optimization_barrier(
        (hidden, normed_partial, stat_partial)
    )
    normed_grad, stats = scatter_channels(normed_partial, stat_partial)
    stats = stats.T
    expand_term = contract_first(normed, pre_grad).reshape(2 * ys, hidden_width, 2, hidden_width)
    expand_grad = scatter_chip_rows(jnp.transpose(expand_term, (2, 0, 1, 3)))
    project_term = contract_first(hidden, grad_panels).reshape(2, hidden_width, 2 * ys, hidden_width)
    project_grad = scatter_chip_rows(jnp.transpose(project_term, (0, 2, 1, 3)))

    partial_out = sum(
        jnp.dot(
            late_hidden[:, g * hidden_width : (g + 1) * hidden_width],
            w_project_chip[g * hidden_width : (g + 1) * hidden_width],
            preferred_element_type=jnp.float32,
        )
        .astype(jnp.bfloat16)
        .astype(jnp.float32)
        for g in range(2)
    )
    projected, _ = scatter_channels(partial_out, jnp.zeros((half, 0)))
    projected = projected + b_project
    residual = image.reshape(positions, channels).astype(jnp.float32)
    result = (
        (residual + layer_scale * projected).astype(jnp.bfloat16).reshape(height, breadth, channels)
    )
    scale_term = jnp.sum(upstream * projected, 0)

    row_stats = chip_blocks(jnp.concatenate([average, inv_std], axis=1), 0)
    gain_part = lax.dynamic_slice_in_dim(norm_gain, channel_start, channels)
    centred_part = (mixed.astype(jnp.float32) - row_stats[:, :1]) * row_stats[:, 1:]
    part_std = row_stats[:, 1:]
    gain_grad = normed_grad * gain_part
    plain_mean = stats[0][:, None] / features
    centred_mean = stats[1][:, None] / features
    mixed_grad = (part_std * (gain_grad - plain_mean - centred_part * centred_mean)).astype(
        jnp.bfloat16
    )
    mixed_grad = mixed_grad.reshape(height, breadth, channels)
    grad_rimmed = extended(mixed_grad, rim_depth)
    wide_grad = jnp.pad(grad_rimmed, ((0, 0), (rim_depth, rim_depth), (0, 0))).astype(jnp.float32)
    back = depthwise(wide_grad, dw_kernel[::-1, ::-1], height, breadth)
    image_grad = (upstream.reshape(height, breadth, channels) + back).astype(jnp.bfloat16)
    kernel_local = kernel_terms(wide_image, mixed_grad.astype(jnp.float32), kernel_size)
    flat = sum_rows(jnp.concatenate([kernel_local.reshape(-1), scale_term]))
    kernel_grad = flat[: kernel_local.size].reshape(kernel_local.shape)
    scale_grad = flat[kernel_local.size :]
    return (result, image_grad, expand_grad, project_grad, kernel_grad, scale_grad)


def solution(mesh):
    tensor_size, rows_size = mesh.devices.shape
    far = 2
    core = 2
    near = 2
    fine = Mesh(
        mesh.devices.reshape(far, tensor_size // (far * core), core, near, rows_size // near),
        ("xh", "z", "c", "xl", "y"),
    )
    return jax.shard_map(
        per_device,
        mesh=fine,
        in_specs=(
            P(ROWS, None, TENSOR),
            P(None, None, TENSOR),
            P(TENSOR),
            P(),
            P(),
            P(ROWS, TENSOR),
            P(TENSOR),
            P(TENSOR, ROWS),
            P(TENSOR),
            P(TENSOR),
            P(ROWS, None, TENSOR),
        ),
        out_specs=(
            P(ROWS, None, TENSOR),
            P(ROWS, None, TENSOR),
            P(ROWS, TENSOR),
            P(TENSOR, ROWS),
            P(None, None, TENSOR),
            P(TENSOR),
        ),
        check_vma=False,
    )
```

```python
import math

import jax
import jax.numpy as jnp
from jax import lax
from jax.sharding import Mesh
from jax.sharding import PartitionSpec as P

EPSILON = 1e-06

TENSOR = ("xh", "z", "c")
ROWS = ("xl", "y")


def shifted(x, axis, count, step):
    return lax.ppermute(x, axis, [(i, (i + step) % count) for i in range(count)])


def order2(mine, other, index):
    first = jnp.where(index == 0, mine, other)
    second = jnp.where(index == 0, other, mine)
    return jnp.stack([first, second])


def ring_gather(x, axis, count, out_axis=0):
    me = lax.axis_index(axis)
    ahead = count // 2
    behind = count - 1 - ahead
    rel = {0: x}
    fwd = x
    for s in range(1, ahead + 1):
        fwd = shifted(fwd, axis, count, 1)
        rel[-s] = fwd
    bwd = x
    for s in range(1, behind + 1):
        bwd = shifted(bwd, axis, count, -1)
        rel[s] = bwd
    placed = jnp.zeros(x.shape[:out_axis] + (count,) + x.shape[out_axis:], x.dtype)
    for k, part in rel.items():
        placed = lax.dynamic_update_index_in_dim(placed, part, (me + k + count) % count, out_axis)
    return placed


def ring_scatter(blocks, axis, count, send_dtype):
    me = lax.axis_index(axis)

    def block(k):
        return lax.dynamic_index_in_dim(blocks, (me + k + count) % count, axis=0, keepdims=False).astype(
            jnp.float32
        )

    ahead = count // 2
    behind = count - 1 - ahead
    total = block(0)
    acc = None
    for s in range(1, ahead + 1):
        part = block(ahead + 1 - s)
        part = part if acc is None else acc + part
        acc = shifted(part.astype(send_dtype), axis, count, 1).astype(jnp.float32)
    total = total + acc
    acc = None
    for s in range(1, behind + 1):
        part = block(-(behind + 1 - s))
        part = part if acc is None else acc + part
        acc = shifted(part.astype(send_dtype), axis, count, -1).astype(jnp.float32)
    if acc is not None:
        total = total + acc
    return total


def gather_channels(x):
    core = lax.axis_index("c")
    far = lax.axis_index("xh")
    kinds, positions, width = x.shape
    half = positions // 2
    own = lax.dynamic_slice_in_dim(x, core * half, half, axis=1)
    sent = lax.dynamic_slice_in_dim(x, (1 - core) * half, half, axis=1)
    got = shifted(sent, "c", 2, 1)
    chip = jnp.concatenate(
        [jnp.where(core == 0, own, got), jnp.where(core == 0, got, own)], axis=2
    )
    other = shifted(chip, "xh", 2, 1)
    pair = jnp.stack(
        [jnp.where(far == 0, chip, other), jnp.where(far == 0, other, chip)], axis=2
    )
    ring = ring_gather(pair, "z", lax.axis_size("z"), 3)
    return ring.reshape(kinds, half, -1)


def scatter_channels(chip, extra):
    core = lax.axis_index("c")
    far = lax.axis_index("xh")
    zs = lax.axis_size("z")
    half, features = chip.shape
    width = features // (4 * zs)
    spread = jnp.broadcast_to(
        extra.astype(jnp.bfloat16)[:, None, None, None, :], (half, 2, zs, 2, extra.shape[1])
    )
    chip = jnp.concatenate([chip.astype(jnp.bfloat16).reshape(half, 2, zs, 2, width), spread], axis=4)
    blocks = jnp.transpose(chip, (2, 0, 1, 3, 4))
    ring = ring_scatter(blocks, "z", zs, jnp.bfloat16)
    mine = lax.dynamic_index_in_dim(ring, far, axis=1, keepdims=False)
    theirs = lax.dynamic_index_in_dim(ring, 1 - far, axis=1, keepdims=False)
    pair = mine + shifted(theirs.astype(jnp.bfloat16), "xh", 2, 1).astype(jnp.float32)
    keep = lax.dynamic_index_in_dim(pair, core, axis=1, keepdims=False)
    give = lax.dynamic_index_in_dim(pair, 1 - core, axis=1, keepdims=False)
    both = by_core(keep, shifted(give, "c", 2, 1), 0)
    return both[:, :width], both[:, width:]


def by_core(mine, other, axis):
    core = lax.axis_index("c")
    return jnp.concatenate(
        [jnp.where(core == 0, mine, other), jnp.where(core == 0, other, mine)], axis=axis
    )


def chip_blocks(x, axis):
    return by_core(x, shifted(x, "c", 2, 1), axis)


def fold_cores(term, axis):
    core = lax.axis_index("c")
    size = term.shape[axis] // 2
    mine = lax.dynamic_slice_in_dim(term, core * size, size, axis=axis)
    give = lax.dynamic_slice_in_dim(term, (1 - core) * size, size, axis=axis)
    return mine + shifted(give.astype(jnp.bfloat16), "c", 2, 1).astype(jnp.float32)


def gather_rows(w, dim):
    return lax.all_gather(w, ROWS, axis=dim, tiled=True)


def scatter_rows(term, dim):
    return lax.psum_scatter(
        term.astype(jnp.bfloat16), ROWS, scatter_dimension=dim, tiled=True
    ).astype(jnp.float32)


def sum_rows(v):
    v = v + shifted(v, "xl", 2, 1)
    return jnp.sum(ring_gather(v, "y", lax.axis_size("y")), axis=0)


def extended(cells, width):
    count = lax.axis_size(ROWS)
    ends = count - 1
    head = lax.slice_in_dim(cells, 0, width, axis=0)
    tail = lax.slice_in_dim(cells, cells.shape[0] - width, cells.shape[0], axis=0)
    return jnp.concatenate(
        [
            lax.ppermute(tail, ROWS, [(i, (i + 1) % count) for i in range(ends)]),
            cells,
            lax.ppermute(head, ROWS, [((i + 1) % count, i) for i in range(ends)]),
        ],
        axis=0,
    )


def gelu_exact(values):
    return 0.5 * values * (1.0 + lax.erf(values * (1.0 / math.sqrt(2.0))))


def gelu_slope(values):
    cumulative = 0.5 * (1.0 + lax.erf(values * (1.0 / math.sqrt(2.0))))
    density = jnp.exp(-0.5 * values * values) * (1.0 / math.sqrt(2.0 * math.pi))
    return cumulative + values * density


def depthwise(padded, kernel, height, breadth):
    kernel_size = kernel.shape[0]
    summed = jnp.zeros((height, breadth, kernel.shape[2]), jnp.float32)
    for row_shift in range(kernel_size):
        for col_shift in range(kernel_size):
            window = padded[row_shift : row_shift + height, col_shift : col_shift + breadth]
            summed = summed + kernel[row_shift, col_shift].astype(jnp.float32) * window
    return summed


def kernel_terms(padded, gradient, kernel_size):
    height, breadth = (gradient.shape[0], gradient.shape[1])
    kernel_rows = []
    for row_shift in range(kernel_size):
        kernel_line = []
        for col_shift in range(kernel_size):
            window = padded[row_shift : row_shift + height, col_shift : col_shift + breadth]
            kernel_line.append(jnp.sum(window * gradient, axis=(0, 1)))
        kernel_rows.append(jnp.stack(kernel_line))
    return jnp.stack(kernel_rows)


def contract_last(left, right):
    return lax.dot_general(
        left, right, (((1,), (1,)), ((), ())), preferred_element_type=jnp.float32
    )


def contract_first(left, right):
    return lax.dot_general(
        left, right, (((0,), (0,)), ((), ())), preferred_element_type=jnp.float32
    )


def per_device(
    image,
    dw_kernel,
    dw_bias,
    norm_gain,
    norm_bias,
    w_expand,
    b_expand,
    w_project,
    b_project,
    layer_scale,
    out_grad,
):
    kernel_size = dw_kernel.shape[0]
    rim_depth = kernel_size // 2
    height, breadth, channels = image.shape
    positions = height * breadth
    features = norm_gain.shape[0]
    channel_start = lax.axis_index(TENSOR) * channels

    core = lax.axis_index("c")
    half = positions // 2
    hidden_width = w_expand.shape[1]
    w_expand_chip = chip_blocks(gather_rows(w_expand, 0), 1)
    w_project_chip = chip_blocks(gather_rows(w_project, 1), 0)
    b_expand_chip = chip_blocks(b_expand, 0)
    upstream = out_grad.reshape(positions, channels).astype(jnp.float32)
    scaled_grad = (upstream * layer_scale).astype(jnp.bfloat16)

    rimmed = extended(image, rim_depth)
    wide_image = jnp.pad(rimmed, ((0, 0), (rim_depth, rim_depth), (0, 0))).astype(jnp.float32)
    convolved = depthwise(wide_image, dw_kernel, height, breadth) + dw_bias
    mixed = convolved.astype(jnp.bfloat16).reshape(positions, channels)
    gathered = gather_channels(jnp.stack([mixed, scaled_grad]))
    all_mixed = gathered[0].astype(jnp.float32)
    grad_panels = gathered[1]
    average = jnp.sum(all_mixed, 1, keepdims=True) / features
    mean_square = jnp.sum(all_mixed * all_mixed, 1, keepdims=True) / features
    inv_std = lax.rsqrt(mean_square - average * average + EPSILON)
    centred = (all_mixed - average) * inv_std
    normed = (centred * norm_gain + norm_bias).astype(jnp.bfloat16)
    pre = jnp.dot(normed, w_expand_chip, preferred_element_type=jnp.float32) + b_expand_chip
    hidden = gelu_exact(pre).astype(jnp.bfloat16)
    hidden_grad = contract_last(grad_panels, w_project_chip)
    pre_grad = (hidden_grad * gelu_slope(pre)).astype(jnp.bfloat16)
    normed_partial = sum(
        contract_last(
            pre_grad[:, g * hidden_width : (g + 1) * hidden_width],
            w_expand_chip[:, g * hidden_width : (g + 1) * hidden_width],
        )
        .astype(jnp.bfloat16)
        .astype(jnp.float32)
        for g in range(2)
    )
    gain_partial = normed_partial * norm_gain
    stat_partial = jnp.stack([jnp.sum(gain_partial, 1), jnp.sum(gain_partial * centred, 1)], axis=1)
    late_hidden, normed_partial, stat_partial = lax.optimization_barrier(
        (hidden, normed_partial, stat_partial)
    )
    normed_grad, stats = scatter_channels(normed_partial, stat_partial)
    stats = stats.T
    expand_grad = scatter_rows(fold_cores(contract_first(normed, pre_grad), 1), 0)
    project_term = fold_cores(contract_first(hidden, grad_panels), 0)
    project_grad = scatter_rows(project_term, 1)

    partial_out = sum(
        jnp.dot(
            late_hidden[:, g * hidden_width : (g + 1) * hidden_width],
            w_project_chip[g * hidden_width : (g + 1) * hidden_width],
            preferred_element_type=jnp.float32,
        )
        .astype(jnp.bfloat16)
        .astype(jnp.float32)
        for g in range(2)
    )
    projected, _ = scatter_channels(partial_out, jnp.zeros((half, 0)))
    projected = projected + b_project
    residual = image.reshape(positions, channels).astype(jnp.float32)
    result = (
        (residual + layer_scale * projected).astype(jnp.bfloat16).reshape(height, breadth, channels)
    )
    scale_term = jnp.sum(upstream * projected, 0)

    row_stats = chip_blocks(jnp.concatenate([average, inv_std], axis=1), 0)
    gain_part = lax.dynamic_slice_in_dim(norm_gain, channel_start, channels)
    centred_part = (mixed.astype(jnp.float32) - row_stats[:, :1]) * row_stats[:, 1:]
    part_std = row_stats[:, 1:]
    gain_grad = normed_grad * gain_part
    plain_mean = stats[0][:, None] / features
    centred_mean = stats[1][:, None] / features
    mixed_grad = (part_std * (gain_grad - plain_mean - centred_part * centred_mean)).astype(
        jnp.bfloat16
    )
    mixed_grad = mixed_grad.reshape(height, breadth, channels)
    grad_rimmed = extended(mixed_grad, rim_depth)
    wide_grad = jnp.pad(grad_rimmed, ((0, 0), (rim_depth, rim_depth), (0, 0))).astype(jnp.float32)
    back = depthwise(wide_grad, dw_kernel[::-1, ::-1], height, breadth)
    image_grad = (upstream.reshape(height, breadth, channels) + back).astype(jnp.bfloat16)
    kernel_local = kernel_terms(wide_image, mixed_grad.astype(jnp.float32), kernel_size)
    flat = sum_rows(jnp.concatenate([kernel_local.reshape(-1), scale_term]))
    kernel_grad = flat[: kernel_local.size].reshape(kernel_local.shape)
    scale_grad = flat[kernel_local.size :]
    return (result, image_grad, expand_grad, project_grad, kernel_grad, scale_grad)


def solution(mesh):
    tensor_size, rows_size = mesh.devices.shape
    far = 2
    core = 2
    near = 2
    fine = Mesh(
        mesh.devices.reshape(far, tensor_size // (far * core), core, near, rows_size // near),
        ("xh", "z", "c", "xl", "y"),
    )
    return jax.shard_map(
        per_device,
        mesh=fine,
        in_specs=(
            P(ROWS, None, TENSOR),
            P(None, None, TENSOR),
            P(TENSOR),
            P(),
            P(),
            P(ROWS, TENSOR),
            P(TENSOR),
            P(TENSOR, ROWS),
            P(TENSOR),
            P(TENSOR),
            P(ROWS, None, TENSOR),
        ),
        out_specs=(
            P(ROWS, None, TENSOR),
            P(ROWS, None, TENSOR),
            P(ROWS, TENSOR),
            P(TENSOR, ROWS),
            P(None, None, TENSOR),
            P(TENSOR),
        ),
        check_vma=False,
    )
```

```python
import math

import jax
import jax.numpy as jnp
from jax import lax
from jax.sharding import Mesh
from jax.sharding import PartitionSpec as P

EPSILON = 1e-06

TENSOR = ("xh", "z", "c")
ROWS = ("xl", "y")


def shifted(x, axis, count, step):
    return lax.ppermute(x, axis, [(i, (i + step) % count) for i in range(count)])


def order2(mine, other, index):
    first = jnp.where(index == 0, mine, other)
    second = jnp.where(index == 0, other, mine)
    return jnp.stack([first, second])


def ring_gather(x, axis, count, out_axis=0):
    me = lax.axis_index(axis)
    ahead = count // 2
    behind = count - 1 - ahead
    rel = {0: x}
    fwd = x
    for s in range(1, ahead + 1):
        fwd = shifted(fwd, axis, count, 1)
        rel[-s] = fwd
    bwd = x
    for s in range(1, behind + 1):
        bwd = shifted(bwd, axis, count, -1)
        rel[s] = bwd
    placed = jnp.zeros(x.shape[:out_axis] + (count,) + x.shape[out_axis:], x.dtype)
    for k, part in rel.items():
        placed = lax.dynamic_update_index_in_dim(placed, part, (me + k + count) % count, out_axis)
    return placed


def ring_scatter(blocks, axis, count, send_dtype):
    me = lax.axis_index(axis)

    def block(k):
        return lax.dynamic_index_in_dim(blocks, (me + k + count) % count, axis=0, keepdims=False).astype(
            jnp.float32
        )

    ahead = count // 2
    behind = count - 1 - ahead
    total = block(0)
    acc = None
    for s in range(1, ahead + 1):
        part = block(ahead + 1 - s)
        part = part if acc is None else acc + part
        acc = shifted(part.astype(send_dtype), axis, count, 1).astype(jnp.float32)
    total = total + acc
    acc = None
    for s in range(1, behind + 1):
        part = block(-(behind + 1 - s))
        part = part if acc is None else acc + part
        acc = shifted(part.astype(send_dtype), axis, count, -1).astype(jnp.float32)
    if acc is not None:
        total = total + acc
    return total


def gather_channels(x):
    core = lax.axis_index("c")
    far = lax.axis_index("xh")
    kinds, positions, width = x.shape
    half = positions // 2
    own = lax.dynamic_slice_in_dim(x, core * half, half, axis=1)
    sent = lax.dynamic_slice_in_dim(x, (1 - core) * half, half, axis=1)
    got = shifted(sent, "c", 2, 1)
    chip = jnp.concatenate(
        [jnp.where(core == 0, own, got), jnp.where(core == 0, got, own)], axis=2
    )
    other = shifted(chip, "xh", 2, 1)
    pair = jnp.stack(
        [jnp.where(far == 0, chip, other), jnp.where(far == 0, other, chip)], axis=2
    )
    ring = ring_gather(pair, "z", lax.axis_size("z"), 3)
    return ring.reshape(kinds, half, -1)


def scatter_channels(chip, extra):
    core = lax.axis_index("c")
    far = lax.axis_index("xh")
    zs = lax.axis_size("z")
    half, features = chip.shape
    width = features // (4 * zs)
    spread = jnp.broadcast_to(
        extra.astype(jnp.bfloat16)[:, None, None, None, :], (half, 2, zs, 2, extra.shape[1])
    )
    chip = jnp.concatenate([chip.astype(jnp.bfloat16).reshape(half, 2, zs, 2, width), spread], axis=4)
    blocks = jnp.transpose(chip, (2, 0, 1, 3, 4))
    ring = ring_scatter(blocks, "z", zs, jnp.bfloat16)
    mine = lax.dynamic_index_in_dim(ring, far, axis=1, keepdims=False)
    theirs = lax.dynamic_index_in_dim(ring, 1 - far, axis=1, keepdims=False)
    pair = mine + shifted(theirs.astype(jnp.bfloat16), "xh", 2, 1).astype(jnp.float32)
    keep = lax.dynamic_index_in_dim(pair, core, axis=1, keepdims=False)
    give = lax.dynamic_index_in_dim(pair, 1 - core, axis=1, keepdims=False)
    both = by_core(keep, shifted(give, "c", 2, 1), 0)
    return both[:, :width], both[:, width:]


def by_core(mine, other, axis):
    core = lax.axis_index("c")
    return jnp.concatenate(
        [jnp.where(core == 0, mine, other), jnp.where(core == 0, other, mine)], axis=axis
    )


def chip_blocks(x, axis):
    return by_core(x, shifted(x, "c", 2, 1), axis)


def fold_cores(term, axis):
    core = lax.axis_index("c")
    size = term.shape[axis] // 2
    mine = lax.dynamic_slice_in_dim(term, core * size, size, axis=axis)
    give = lax.dynamic_slice_in_dim(term, (1 - core) * size, size, axis=axis)
    return mine + shifted(give.astype(jnp.bfloat16), "c", 2, 1).astype(jnp.float32)


def gather_rows(w, dim):
    return lax.all_gather(w, ROWS, axis=dim, tiled=True)


def scatter_rows(term, dim):
    return lax.psum_scatter(
        term.astype(jnp.bfloat16), ROWS, scatter_dimension=dim, tiled=True
    ).astype(jnp.float32)


def sum_rows(v):
    v = v + shifted(v, "xl", 2, 1)
    return jnp.sum(ring_gather(v, "y", lax.axis_size("y")), axis=0)


def extended(cells, width):
    count = lax.axis_size(ROWS)
    ends = count - 1
    head = lax.slice_in_dim(cells, 0, width, axis=0)
    tail = lax.slice_in_dim(cells, cells.shape[0] - width, cells.shape[0], axis=0)
    return jnp.concatenate(
        [
            lax.ppermute(tail, ROWS, [(i, (i + 1) % count) for i in range(ends)]),
            cells,
            lax.ppermute(head, ROWS, [((i + 1) % count, i) for i in range(ends)]),
        ],
        axis=0,
    )


def gelu_exact(values):
    return 0.5 * values * (1.0 + lax.erf(values * (1.0 / math.sqrt(2.0))))


def gelu_slope(values):
    cumulative = 0.5 * (1.0 + lax.erf(values * (1.0 / math.sqrt(2.0))))
    density = jnp.exp(-0.5 * values * values) * (1.0 / math.sqrt(2.0 * math.pi))
    return cumulative + values * density


def depthwise(padded, kernel, height, breadth):
    kernel_size = kernel.shape[0]
    summed = jnp.zeros((height, breadth, kernel.shape[2]), jnp.float32)
    for row_shift in range(kernel_size):
        for col_shift in range(kernel_size):
            window = padded[row_shift : row_shift + height, col_shift : col_shift + breadth]
            summed = summed + kernel[row_shift, col_shift].astype(jnp.float32) * window
    return summed


def kernel_terms(padded, gradient, kernel_size):
    height, breadth = (gradient.shape[0], gradient.shape[1])
    kernel_rows = []
    for row_shift in range(kernel_size):
        kernel_line = []
        for col_shift in range(kernel_size):
            window = padded[row_shift : row_shift + height, col_shift : col_shift + breadth]
            kernel_line.append(jnp.sum(window * gradient, axis=(0, 1)))
        kernel_rows.append(jnp.stack(kernel_line))
    return jnp.stack(kernel_rows)


def contract_last(left, right):
    return lax.dot_general(
        left, right, (((1,), (1,)), ((), ())), preferred_element_type=jnp.float32
    )


def contract_first(left, right):
    return lax.dot_general(
        left, right, (((0,), (0,)), ((), ())), preferred_element_type=jnp.float32
    )


def per_device(
    image,
    dw_kernel,
    dw_bias,
    norm_gain,
    norm_bias,
    w_expand,
    b_expand,
    w_project,
    b_project,
    layer_scale,
    out_grad,
):
    kernel_size = dw_kernel.shape[0]
    rim_depth = kernel_size // 2
    height, breadth, channels = image.shape
    positions = height * breadth
    features = norm_gain.shape[0]
    channel_start = lax.axis_index(TENSOR) * channels

    core = lax.axis_index("c")
    half = positions // 2
    hidden_width = w_expand.shape[1]
    w_expand_chip = chip_blocks(gather_rows(w_expand, 0), 1)
    w_project_chip = chip_blocks(gather_rows(w_project, 1), 0)
    b_expand_chip = chip_blocks(b_expand, 0)
    upstream = out_grad.reshape(positions, channels).astype(jnp.float32)
    scaled_grad = (upstream * layer_scale).astype(jnp.bfloat16)

    rimmed = extended(image, rim_depth)
    wide_image = jnp.pad(rimmed, ((0, 0), (rim_depth, rim_depth), (0, 0))).astype(jnp.float32)
    convolved = depthwise(wide_image, dw_kernel, height, breadth) + dw_bias
    mixed = convolved.astype(jnp.bfloat16).reshape(positions, channels)
    gathered = gather_channels(jnp.stack([mixed, scaled_grad]))
    all_mixed = gathered[0].astype(jnp.float32)
    grad_panels = gathered[1]
    average = jnp.sum(all_mixed, 1, keepdims=True) / features
    mean_square = jnp.sum(all_mixed * all_mixed, 1, keepdims=True) / features
    inv_std = lax.rsqrt(mean_square - average * average + EPSILON)
    centred = (all_mixed - average) * inv_std
    normed = (centred * norm_gain + norm_bias).astype(jnp.bfloat16)
    pre = jnp.dot(normed, w_expand_chip, preferred_element_type=jnp.float32) + b_expand_chip
    hidden = gelu_exact(pre).astype(jnp.bfloat16)
    hidden_grad = contract_last(grad_panels, w_project_chip)
    pre_grad = (hidden_grad * gelu_slope(pre)).astype(jnp.bfloat16)
    normed_partial = sum(
        contract_last(
            pre_grad[:, g * hidden_width : (g + 1) * hidden_width],
            w_expand_chip[:, g * hidden_width : (g + 1) * hidden_width],
        )
        .astype(jnp.bfloat16)
        .astype(jnp.float32)
        for g in range(2)
    )
    gain_partial = normed_partial * norm_gain
    stat_partial = jnp.stack([jnp.sum(gain_partial, 1), jnp.sum(gain_partial * centred, 1)], axis=1)
    late_hidden, normed_partial, stat_partial = lax.optimization_barrier(
        (hidden, normed_partial, stat_partial)
    )
    normed_grad, stats = scatter_channels(normed_partial, stat_partial)
    stats = stats.T
    expand_grad = scatter_rows(fold_cores(contract_first(normed, pre_grad), 1), 0)
    project_term = fold_cores(contract_first(grad_panels, hidden), 1)
    project_grad = scatter_rows(project_term, 0).T

    partial_out = sum(
        jnp.dot(
            late_hidden[:, g * hidden_width : (g + 1) * hidden_width],
            w_project_chip[g * hidden_width : (g + 1) * hidden_width],
            preferred_element_type=jnp.float32,
        )
        .astype(jnp.bfloat16)
        .astype(jnp.float32)
        for g in range(2)
    )
    projected, _ = scatter_channels(partial_out, jnp.zeros((half, 0)))
    projected = projected + b_project
    residual = image.reshape(positions, channels).astype(jnp.float32)
    result = (
        (residual + layer_scale * projected).astype(jnp.bfloat16).reshape(height, breadth, channels)
    )
    scale_term = jnp.sum(upstream * projected, 0)

    row_stats = chip_blocks(jnp.concatenate([average, inv_std], axis=1), 0)
    gain_part = lax.dynamic_slice_in_dim(norm_gain, channel_start, channels)
    centred_part = (mixed.astype(jnp.float32) - row_stats[:, :1]) * row_stats[:, 1:]
    part_std = row_stats[:, 1:]
    gain_grad = normed_grad * gain_part
    plain_mean = stats[0][:, None] / features
    centred_mean = stats[1][:, None] / features
    mixed_grad = (part_std * (gain_grad - plain_mean - centred_part * centred_mean)).astype(
        jnp.bfloat16
    )
    mixed_grad = mixed_grad.reshape(height, breadth, channels)
    grad_rimmed = extended(mixed_grad, rim_depth)
    wide_grad = jnp.pad(grad_rimmed, ((0, 0), (rim_depth, rim_depth), (0, 0))).astype(jnp.float32)
    back = depthwise(wide_grad, dw_kernel[::-1, ::-1], height, breadth)
    image_grad = (upstream.reshape(height, breadth, channels) + back).astype(jnp.bfloat16)
    kernel_local = kernel_terms(wide_image, mixed_grad.astype(jnp.float32), kernel_size)
    flat = sum_rows(jnp.concatenate([kernel_local.reshape(-1), scale_term]))
    kernel_grad = flat[: kernel_local.size].reshape(kernel_local.shape)
    scale_grad = flat[kernel_local.size :]
    return (result, image_grad, expand_grad, project_grad, kernel_grad, scale_grad)


def solution(mesh):
    tensor_size, rows_size = mesh.devices.shape
    far = 2
    core = 2
    near = 2
    fine = Mesh(
        mesh.devices.reshape(far, tensor_size // (far * core), core, near, rows_size // near),
        ("xh", "z", "c", "xl", "y"),
    )
    return jax.shard_map(
        per_device,
        mesh=fine,
        in_specs=(
            P(ROWS, None, TENSOR),
            P(None, None, TENSOR),
            P(TENSOR),
            P(),
            P(),
            P(ROWS, TENSOR),
            P(TENSOR),
            P(TENSOR, ROWS),
            P(TENSOR),
            P(TENSOR),
            P(ROWS, None, TENSOR),
        ),
        out_specs=(
            P(ROWS, None, TENSOR),
            P(ROWS, None, TENSOR),
            P(ROWS, TENSOR),
            P(TENSOR, ROWS),
            P(None, None, TENSOR),
            P(TENSOR),
        ),
        check_vma=False,
    )
```

```python
import math

import jax
import jax.numpy as jnp
from jax import lax
from jax.sharding import Mesh
from jax.sharding import PartitionSpec as P

EPSILON = 1e-06

TENSOR = ("xh", "z", "c")
ROWS = ("xl", "y")


def shifted(x, axis, count, step):
    return lax.ppermute(x, axis, [(i, (i + step) % count) for i in range(count)])


def order2(mine, other, index):
    first = jnp.where(index == 0, mine, other)
    second = jnp.where(index == 0, other, mine)
    return jnp.stack([first, second])


def ring_gather(x, axis, count, out_axis=0):
    me = lax.axis_index(axis)
    ahead = count // 2
    behind = count - 1 - ahead
    rel = {0: x}
    fwd = x
    for s in range(1, ahead + 1):
        fwd = shifted(fwd, axis, count, 1)
        rel[-s] = fwd
    bwd = x
    for s in range(1, behind + 1):
        bwd = shifted(bwd, axis, count, -1)
        rel[s] = bwd
    placed = jnp.zeros(x.shape[:out_axis] + (count,) + x.shape[out_axis:], x.dtype)
    for k, part in rel.items():
        placed = lax.dynamic_update_index_in_dim(placed, part, (me + k + count) % count, out_axis)
    return placed


def ring_scatter(blocks, axis, count, send_dtype):
    me = lax.axis_index(axis)

    def block(k):
        return lax.dynamic_index_in_dim(blocks, (me + k + count) % count, axis=0, keepdims=False).astype(
            jnp.float32
        )

    ahead = count // 2
    behind = count - 1 - ahead
    total = block(0)
    acc = None
    for s in range(1, ahead + 1):
        part = block(ahead + 1 - s)
        part = part if acc is None else acc + part
        acc = shifted(part.astype(send_dtype), axis, count, 1).astype(jnp.float32)
    total = total + acc
    acc = None
    for s in range(1, behind + 1):
        part = block(-(behind + 1 - s))
        part = part if acc is None else acc + part
        acc = shifted(part.astype(send_dtype), axis, count, -1).astype(jnp.float32)
    if acc is not None:
        total = total + acc
    return total


def gather_channels(x):
    core = lax.axis_index("c")
    far = lax.axis_index("xh")
    kinds, positions, width = x.shape
    half = positions // 2
    own = lax.dynamic_slice_in_dim(x, core * half, half, axis=1)
    sent = lax.dynamic_slice_in_dim(x, (1 - core) * half, half, axis=1)
    got = shifted(sent, "c", 2, 1)
    chip = jnp.concatenate(
        [jnp.where(core == 0, own, got), jnp.where(core == 0, got, own)], axis=2
    )
    other = shifted(chip, "xh", 2, 1)
    pair = jnp.stack(
        [jnp.where(far == 0, chip, other), jnp.where(far == 0, other, chip)], axis=2
    )
    ring = ring_gather(pair, "z", lax.axis_size("z"), 3)
    return ring.reshape(kinds, half, -1)


def scatter_channels(chip, extra):
    core = lax.axis_index("c")
    far = lax.axis_index("xh")
    zs = lax.axis_size("z")
    half, features = chip.shape
    width = features // (4 * zs)
    spread = jnp.broadcast_to(
        extra.astype(jnp.bfloat16)[:, None, None, None, :], (half, 2, zs, 2, extra.shape[1])
    )
    chip = jnp.concatenate([chip.astype(jnp.bfloat16).reshape(half, 2, zs, 2, width), spread], axis=4)
    blocks = jnp.transpose(chip, (2, 0, 1, 3, 4))
    ring = ring_scatter(blocks, "z", zs, jnp.bfloat16)
    mine = lax.dynamic_index_in_dim(ring, far, axis=1, keepdims=False)
    theirs = lax.dynamic_index_in_dim(ring, 1 - far, axis=1, keepdims=False)
    pair = mine + shifted(theirs.astype(jnp.bfloat16), "xh", 2, 1).astype(jnp.float32)
    keep = lax.dynamic_index_in_dim(pair, core, axis=1, keepdims=False)
    give = lax.dynamic_index_in_dim(pair, 1 - core, axis=1, keepdims=False)
    both = by_core(keep, shifted(give, "c", 2, 1), 0)
    return both[:, :width], both[:, width:]


def by_core(mine, other, axis):
    core = lax.axis_index("c")
    return jnp.concatenate(
        [jnp.where(core == 0, mine, other), jnp.where(core == 0, other, mine)], axis=axis
    )


def chip_blocks(x, axis):
    return by_core(x, shifted(x, "c", 2, 1), axis)


def fold_cores(term, axis):
    core = lax.axis_index("c")
    size = term.shape[axis] // 2
    mine = lax.dynamic_slice_in_dim(term, core * size, size, axis=axis)
    give = lax.dynamic_slice_in_dim(term, (1 - core) * size, size, axis=axis)
    return mine + shifted(give.astype(jnp.bfloat16), "c", 2, 1).astype(jnp.float32)


def gather_rows(w, dim):
    return lax.all_gather(w, ROWS, axis=dim, tiled=True)


def scatter_rows(term, dim):
    return lax.psum_scatter(
        term.astype(jnp.bfloat16), ROWS, scatter_dimension=dim, tiled=True
    ).astype(jnp.float32)


def ring_scatter_rows(term, dim):
    ys = lax.axis_size("y")
    term = jnp.moveaxis(term, dim, 0)
    rest = term.shape[1:]
    block = term.shape[0] // (2 * ys)
    term = term.reshape((2, ys, block) + rest)
    part = ring_scatter(jnp.swapaxes(term, 0, 1), "y", ys, jnp.bfloat16)
    part = ring_scatter(part, "xl", 2, jnp.bfloat16)
    return jnp.moveaxis(part, 0, dim)


def sum_rows(v):
    v = v + shifted(v, "xl", 2, 1)
    return jnp.sum(ring_gather(v, "y", lax.axis_size("y")), axis=0)


def extended(cells, width):
    count = lax.axis_size(ROWS)
    ends = count - 1
    head = lax.slice_in_dim(cells, 0, width, axis=0)
    tail = lax.slice_in_dim(cells, cells.shape[0] - width, cells.shape[0], axis=0)
    return jnp.concatenate(
        [
            lax.ppermute(tail, ROWS, [(i, (i + 1) % count) for i in range(ends)]),
            cells,
            lax.ppermute(head, ROWS, [((i + 1) % count, i) for i in range(ends)]),
        ],
        axis=0,
    )


def gelu_exact(values):
    return 0.5 * values * (1.0 + lax.erf(values * (1.0 / math.sqrt(2.0))))


def gelu_slope(values):
    cumulative = 0.5 * (1.0 + lax.erf(values * (1.0 / math.sqrt(2.0))))
    density = jnp.exp(-0.5 * values * values) * (1.0 / math.sqrt(2.0 * math.pi))
    return cumulative + values * density


def depthwise(padded, kernel, height, breadth):
    kernel_size = kernel.shape[0]
    summed = jnp.zeros((height, breadth, kernel.shape[2]), jnp.float32)
    for row_shift in range(kernel_size):
        for col_shift in range(kernel_size):
            window = padded[row_shift : row_shift + height, col_shift : col_shift + breadth]
            summed = summed + kernel[row_shift, col_shift].astype(jnp.float32) * window
    return summed


def kernel_terms(padded, gradient, kernel_size):
    height, breadth = (gradient.shape[0], gradient.shape[1])
    kernel_rows = []
    for row_shift in range(kernel_size):
        kernel_line = []
        for col_shift in range(kernel_size):
            window = padded[row_shift : row_shift + height, col_shift : col_shift + breadth]
            kernel_line.append(jnp.sum(window * gradient, axis=(0, 1)))
        kernel_rows.append(jnp.stack(kernel_line))
    return jnp.stack(kernel_rows)


def contract_last(left, right):
    return lax.dot_general(
        left, right, (((1,), (1,)), ((), ())), preferred_element_type=jnp.float32
    )


def contract_first(left, right):
    return lax.dot_general(
        left, right, (((0,), (0,)), ((), ())), preferred_element_type=jnp.float32
    )


def per_device(
    image,
    dw_kernel,
    dw_bias,
    norm_gain,
    norm_bias,
    w_expand,
    b_expand,
    w_project,
    b_project,
    layer_scale,
    out_grad,
):
    kernel_size = dw_kernel.shape[0]
    rim_depth = kernel_size // 2
    height, breadth, channels = image.shape
    positions = height * breadth
    features = norm_gain.shape[0]
    channel_start = lax.axis_index(TENSOR) * channels

    core = lax.axis_index("c")
    half = positions // 2
    hidden_width = w_expand.shape[1]
    w_expand_chip = chip_blocks(gather_rows(w_expand, 0), 1)
    w_project_chip = chip_blocks(gather_rows(w_project, 1), 0)
    b_expand_chip = chip_blocks(b_expand, 0)
    upstream = out_grad.reshape(positions, channels).astype(jnp.float32)
    scaled_grad = (upstream * layer_scale).astype(jnp.bfloat16)

    rimmed = extended(image, rim_depth)
    wide_image = jnp.pad(rimmed, ((0, 0), (rim_depth, rim_depth), (0, 0))).astype(jnp.float32)
    convolved = depthwise(wide_image, dw_kernel, height, breadth) + dw_bias
    mixed = convolved.astype(jnp.bfloat16).reshape(positions, channels)
    gathered = gather_channels(jnp.stack([mixed, scaled_grad]))
    all_mixed = gathered[0].astype(jnp.float32)
    grad_panels = gathered[1]
    average = jnp.sum(all_mixed, 1, keepdims=True) / features
    mean_square = jnp.sum(all_mixed * all_mixed, 1, keepdims=True) / features
    inv_std = lax.rsqrt(mean_square - average * average + EPSILON)
    centred = (all_mixed - average) * inv_std
    normed = (centred * norm_gain + norm_bias).astype(jnp.bfloat16)
    pre = jnp.dot(normed, w_expand_chip, preferred_element_type=jnp.float32) + b_expand_chip
    hidden = gelu_exact(pre).astype(jnp.bfloat16)
    hidden_grad = contract_last(grad_panels, w_project_chip)
    pre_grad = (hidden_grad * gelu_slope(pre)).astype(jnp.bfloat16)
    normed_partial = sum(
        contract_last(
            pre_grad[:, g * hidden_width : (g + 1) * hidden_width],
            w_expand_chip[:, g * hidden_width : (g + 1) * hidden_width],
        )
        .astype(jnp.bfloat16)
        .astype(jnp.float32)
        for g in range(2)
    )
    gain_partial = normed_partial * norm_gain
    stat_partial = jnp.stack([jnp.sum(gain_partial, 1), jnp.sum(gain_partial * centred, 1)], axis=1)
    late_hidden, normed_partial, stat_partial = lax.optimization_barrier(
        (hidden, normed_partial, stat_partial)
    )
    normed_grad, stats = scatter_channels(normed_partial, stat_partial)
    stats = stats.T
    expand_grad = ring_scatter_rows(fold_cores(contract_first(normed, pre_grad), 1), 0)
    project_term = fold_cores(contract_first(hidden, grad_panels), 0)
    project_grad = scatter_rows(project_term, 1)

    partial_out = sum(
        jnp.dot(
            late_hidden[:, g * hidden_width : (g + 1) * hidden_width],
            w_project_chip[g * hidden_width : (g + 1) * hidden_width],
            preferred_element_type=jnp.float32,
        )
        .astype(jnp.bfloat16)
        .astype(jnp.float32)
        for g in range(2)
    )
    projected, _ = scatter_channels(partial_out, jnp.zeros((half, 0)))
    projected = projected + b_project
    residual = image.reshape(positions, channels).astype(jnp.float32)
    result = (
        (residual + layer_scale * projected).astype(jnp.bfloat16).reshape(height, breadth, channels)
    )
    scale_term = jnp.sum(upstream * projected, 0)

    row_stats = chip_blocks(jnp.concatenate([average, inv_std], axis=1), 0)
    gain_part = lax.dynamic_slice_in_dim(norm_gain, channel_start, channels)
    centred_part = (mixed.astype(jnp.float32) - row_stats[:, :1]) * row_stats[:, 1:]
    part_std = row_stats[:, 1:]
    gain_grad = normed_grad * gain_part
    plain_mean = stats[0][:, None] / features
    centred_mean = stats[1][:, None] / features
    mixed_grad = (part_std * (gain_grad - plain_mean - centred_part * centred_mean)).astype(
        jnp.bfloat16
    )
    mixed_grad = mixed_grad.reshape(height, breadth, channels)
    grad_rimmed = extended(mixed_grad, rim_depth)
    wide_grad = jnp.pad(grad_rimmed, ((0, 0), (rim_depth, rim_depth), (0, 0))).astype(jnp.float32)
    back = depthwise(wide_grad, dw_kernel[::-1, ::-1], height, breadth)
    image_grad = (upstream.reshape(height, breadth, channels) + back).astype(jnp.bfloat16)
    kernel_local = kernel_terms(wide_image, mixed_grad.astype(jnp.float32), kernel_size)
    flat = sum_rows(jnp.concatenate([kernel_local.reshape(-1), scale_term]))
    kernel_grad = flat[: kernel_local.size].reshape(kernel_local.shape)
    scale_grad = flat[kernel_local.size :]
    return (result, image_grad, expand_grad, project_grad, kernel_grad, scale_grad)


def solution(mesh):
    tensor_size, rows_size = mesh.devices.shape
    far = 2
    core = 2
    near = 2
    fine = Mesh(
        mesh.devices.reshape(far, tensor_size // (far * core), core, near, rows_size // near),
        ("xh", "z", "c", "xl", "y"),
    )
    return jax.shard_map(
        per_device,
        mesh=fine,
        in_specs=(
            P(ROWS, None, TENSOR),
            P(None, None, TENSOR),
            P(TENSOR),
            P(),
            P(),
            P(ROWS, TENSOR),
            P(TENSOR),
            P(TENSOR, ROWS),
            P(TENSOR),
            P(TENSOR),
            P(ROWS, None, TENSOR),
        ),
        out_specs=(
            P(ROWS, None, TENSOR),
            P(ROWS, None, TENSOR),
            P(ROWS, TENSOR),
            P(TENSOR, ROWS),
            P(None, None, TENSOR),
            P(TENSOR),
        ),
        check_vma=False,
    )
```

```python
import math

import jax
import jax.numpy as jnp
from jax import lax
from jax.sharding import Mesh
from jax.sharding import PartitionSpec as P

EPSILON = 1e-06

TENSOR = ("xh", "z", "c")
ROWS = ("xl", "y")


def shifted(x, axis, count, step):
    return lax.ppermute(x, axis, [(i, (i + step) % count) for i in range(count)])


def order2(mine, other, index):
    first = jnp.where(index == 0, mine, other)
    second = jnp.where(index == 0, other, mine)
    return jnp.stack([first, second])


def ring_gather(x, axis, count, out_axis=0):
    me = lax.axis_index(axis)
    ahead = count // 2
    behind = count - 1 - ahead
    rel = {0: x}
    fwd = x
    for s in range(1, ahead + 1):
        fwd = shifted(fwd, axis, count, 1)
        rel[-s] = fwd
    bwd = x
    for s in range(1, behind + 1):
        bwd = shifted(bwd, axis, count, -1)
        rel[s] = bwd
    placed = jnp.zeros(x.shape[:out_axis] + (count,) + x.shape[out_axis:], x.dtype)
    for k, part in rel.items():
        placed = lax.dynamic_update_index_in_dim(placed, part, (me + k + count) % count, out_axis)
    return placed


def ring_scatter(blocks, axis, count, send_dtype):
    me = lax.axis_index(axis)

    def block(k):
        return lax.dynamic_index_in_dim(blocks, (me + k + count) % count, axis=0, keepdims=False).astype(
            jnp.float32
        )

    ahead = count // 2
    behind = count - 1 - ahead
    total = block(0)
    acc = None
    for s in range(1, ahead + 1):
        part = block(ahead + 1 - s)
        part = part if acc is None else acc + part
        acc = shifted(part.astype(send_dtype), axis, count, 1).astype(jnp.float32)
    total = total + acc
    acc = None
    for s in range(1, behind + 1):
        part = block(-(behind + 1 - s))
        part = part if acc is None else acc + part
        acc = shifted(part.astype(send_dtype), axis, count, -1).astype(jnp.float32)
    if acc is not None:
        total = total + acc
    return total


def gather_channels(x):
    core = lax.axis_index("c")
    far = lax.axis_index("xh")
    kinds, positions, width = x.shape
    half = positions // 2
    own = lax.dynamic_slice_in_dim(x, core * half, half, axis=1)
    sent = lax.dynamic_slice_in_dim(x, (1 - core) * half, half, axis=1)
    got = shifted(sent, "c", 2, 1)
    chip = jnp.concatenate(
        [jnp.where(core == 0, own, got), jnp.where(core == 0, got, own)], axis=2
    )
    other = shifted(chip, "xh", 2, 1)
    pair = jnp.stack(
        [jnp.where(far == 0, chip, other), jnp.where(far == 0, other, chip)], axis=2
    )
    ring = ring_gather(pair, "z", lax.axis_size("z"), 3)
    return ring.reshape(kinds, half, -1)


def scatter_channels(chip, extra):
    core = lax.axis_index("c")
    far = lax.axis_index("xh")
    zs = lax.axis_size("z")
    half, features = chip.shape
    width = features // (4 * zs)
    spread = jnp.broadcast_to(
        extra.astype(jnp.bfloat16)[:, None, None, None, :], (half, 2, zs, 2, extra.shape[1])
    )
    chip = jnp.concatenate([chip.astype(jnp.bfloat16).reshape(half, 2, zs, 2, width), spread], axis=4)
    blocks = jnp.transpose(chip, (2, 0, 1, 3, 4))
    ring = ring_scatter(blocks, "z", zs, jnp.bfloat16)
    mine = lax.dynamic_index_in_dim(ring, far, axis=1, keepdims=False)
    theirs = lax.dynamic_index_in_dim(ring, 1 - far, axis=1, keepdims=False)
    pair = mine + shifted(theirs.astype(jnp.bfloat16), "xh", 2, 1).astype(jnp.float32)
    keep = lax.dynamic_index_in_dim(pair, core, axis=1, keepdims=False)
    give = lax.dynamic_index_in_dim(pair, 1 - core, axis=1, keepdims=False)
    both = by_core(keep, shifted(give.astype(jnp.bfloat16), "c", 2, 1).astype(jnp.float32), 0)
    return both[:, :width], both[:, width:]


def by_core(mine, other, axis):
    core = lax.axis_index("c")
    return jnp.concatenate(
        [jnp.where(core == 0, mine, other), jnp.where(core == 0, other, mine)], axis=axis
    )


def chip_blocks(x, axis):
    return by_core(x, shifted(x, "c", 2, 1), axis)


def fold_cores(term, axis):
    core = lax.axis_index("c")
    size = term.shape[axis] // 2
    mine = lax.dynamic_slice_in_dim(term, core * size, size, axis=axis)
    give = lax.dynamic_slice_in_dim(term, (1 - core) * size, size, axis=axis)
    return mine + shifted(give.astype(jnp.bfloat16), "c", 2, 1).astype(jnp.float32)


def gather_rows(w, dim):
    return lax.all_gather(w, ROWS, axis=dim, tiled=True)


def scatter_rows(term, dim):
    return lax.psum_scatter(
        term.astype(jnp.bfloat16), ROWS, scatter_dimension=dim, tiled=True
    ).astype(jnp.float32)


def sum_rows(v):
    v = v + shifted(v, "xl", 2, 1)
    return jnp.sum(ring_gather(v, "y", lax.axis_size("y")), axis=0)


def extended(cells, width):
    count = lax.axis_size(ROWS)
    ends = count - 1
    head = lax.slice_in_dim(cells, 0, width, axis=0)
    tail = lax.slice_in_dim(cells, cells.shape[0] - width, cells.shape[0], axis=0)
    return jnp.concatenate(
        [
            lax.ppermute(tail, ROWS, [(i, (i + 1) % count) for i in range(ends)]),
            cells,
            lax.ppermute(head, ROWS, [((i + 1) % count, i) for i in range(ends)]),
        ],
        axis=0,
    )


def gelu_exact(values):
    return 0.5 * values * (1.0 + lax.erf(values * (1.0 / math.sqrt(2.0))))


def gelu_slope(values):
    cumulative = 0.5 * (1.0 + lax.erf(values * (1.0 / math.sqrt(2.0))))
    density = jnp.exp(-0.5 * values * values) * (1.0 / math.sqrt(2.0 * math.pi))
    return cumulative + values * density


def depthwise(padded, kernel, height, breadth):
    kernel_size = kernel.shape[0]
    summed = jnp.zeros((height, breadth, kernel.shape[2]), jnp.float32)
    for row_shift in range(kernel_size):
        for col_shift in range(kernel_size):
            window = padded[row_shift : row_shift + height, col_shift : col_shift + breadth]
            summed = summed + kernel[row_shift, col_shift].astype(jnp.float32) * window
    return summed


def kernel_terms(padded, gradient, kernel_size):
    height, breadth = (gradient.shape[0], gradient.shape[1])
    kernel_rows = []
    for row_shift in range(kernel_size):
        kernel_line = []
        for col_shift in range(kernel_size):
            window = padded[row_shift : row_shift + height, col_shift : col_shift + breadth]
            kernel_line.append(jnp.sum(window * gradient, axis=(0, 1)))
        kernel_rows.append(jnp.stack(kernel_line))
    return jnp.stack(kernel_rows)


def contract_last(left, right):
    return lax.dot_general(
        left, right, (((1,), (1,)), ((), ())), preferred_element_type=jnp.float32
    )


def contract_first(left, right):
    return lax.dot_general(
        left, right, (((0,), (0,)), ((), ())), preferred_element_type=jnp.float32
    )


def per_device(
    image,
    dw_kernel,
    dw_bias,
    norm_gain,
    norm_bias,
    w_expand,
    b_expand,
    w_project,
    b_project,
    layer_scale,
    out_grad,
):
    kernel_size = dw_kernel.shape[0]
    rim_depth = kernel_size // 2
    height, breadth, channels = image.shape
    positions = height * breadth
    features = norm_gain.shape[0]
    channel_start = lax.axis_index(TENSOR) * channels

    core = lax.axis_index("c")
    half = positions // 2
    hidden_width = w_expand.shape[1]
    w_expand_chip = chip_blocks(gather_rows(w_expand, 0), 1)
    w_project_chip = chip_blocks(gather_rows(w_project, 1), 0)
    b_expand_chip = chip_blocks(b_expand, 0)
    upstream = out_grad.reshape(positions, channels).astype(jnp.float32)
    scaled_grad = (upstream * layer_scale).astype(jnp.bfloat16)

    rimmed = extended(image, rim_depth)
    wide_image = jnp.pad(rimmed, ((0, 0), (rim_depth, rim_depth), (0, 0))).astype(jnp.float32)
    convolved = depthwise(wide_image, dw_kernel, height, breadth) + dw_bias
    mixed = convolved.astype(jnp.bfloat16).reshape(positions, channels)
    gathered = gather_channels(jnp.stack([mixed, scaled_grad]))
    all_mixed = gathered[0].astype(jnp.float32)
    grad_panels = gathered[1]
    average = jnp.sum(all_mixed, 1, keepdims=True) / features
    mean_square = jnp.sum(all_mixed * all_mixed, 1, keepdims=True) / features
    inv_std = lax.rsqrt(mean_square - average * average + EPSILON)
    centred = (all_mixed - average) * inv_std
    normed = (centred * norm_gain + norm_bias).astype(jnp.bfloat16)
    pre = jnp.dot(normed, w_expand_chip, preferred_element_type=jnp.float32) + b_expand_chip
    hidden = gelu_exact(pre).astype(jnp.bfloat16)
    hidden_grad = contract_last(grad_panels, w_project_chip)
    pre_grad = (hidden_grad * gelu_slope(pre)).astype(jnp.bfloat16)
    normed_partial = sum(
        contract_last(
            pre_grad[:, g * hidden_width : (g + 1) * hidden_width],
            w_expand_chip[:, g * hidden_width : (g + 1) * hidden_width],
        )
        .astype(jnp.bfloat16)
        .astype(jnp.float32)
        for g in range(2)
    )
    gain_partial = normed_partial * norm_gain
    stat_partial = jnp.stack([jnp.sum(gain_partial, 1), jnp.sum(gain_partial * centred, 1)], axis=1)
    late_hidden, normed_partial, stat_partial = lax.optimization_barrier(
        (hidden, normed_partial, stat_partial)
    )
    normed_grad, stats = scatter_channels(normed_partial, stat_partial)
    stats = stats.T
    expand_grad = scatter_rows(fold_cores(contract_first(normed, pre_grad), 1), 0)
    project_term = fold_cores(contract_first(hidden, grad_panels), 0)
    project_grad = scatter_rows(project_term, 1)

    partial_out = sum(
        jnp.dot(
            late_hidden[:, g * hidden_width : (g + 1) * hidden_width],
            w_project_chip[g * hidden_width : (g + 1) * hidden_width],
            preferred_element_type=jnp.float32,
        )
        .astype(jnp.bfloat16)
        .astype(jnp.float32)
        for g in range(2)
    )
    projected, _ = scatter_channels(partial_out, jnp.zeros((half, 0)))
    projected = projected + b_project
    residual = image.reshape(positions, channels).astype(jnp.float32)
    result = (
        (residual + layer_scale * projected).astype(jnp.bfloat16).reshape(height, breadth, channels)
    )
    scale_term = jnp.sum(upstream * projected, 0)

    row_stats = chip_blocks(jnp.concatenate([average, inv_std], axis=1), 0)
    gain_part = lax.dynamic_slice_in_dim(norm_gain, channel_start, channels)
    centred_part = (mixed.astype(jnp.float32) - row_stats[:, :1]) * row_stats[:, 1:]
    part_std = row_stats[:, 1:]
    gain_grad = normed_grad * gain_part
    plain_mean = stats[0][:, None] / features
    centred_mean = stats[1][:, None] / features
    mixed_grad = (part_std * (gain_grad - plain_mean - centred_part * centred_mean)).astype(
        jnp.bfloat16
    )
    mixed_grad = mixed_grad.reshape(height, breadth, channels)
    grad_rimmed = extended(mixed_grad, rim_depth)
    wide_grad = jnp.pad(grad_rimmed, ((0, 0), (rim_depth, rim_depth), (0, 0))).astype(jnp.float32)
    back = depthwise(wide_grad, dw_kernel[::-1, ::-1], height, breadth)
    image_grad = (upstream.reshape(height, breadth, channels) + back).astype(jnp.bfloat16)
    kernel_local = kernel_terms(wide_image, mixed_grad.astype(jnp.float32), kernel_size)
    flat = sum_rows(jnp.concatenate([kernel_local.reshape(-1), scale_term]))
    kernel_grad = flat[: kernel_local.size].reshape(kernel_local.shape)
    scale_grad = flat[kernel_local.size :]
    return (result, image_grad, expand_grad, project_grad, kernel_grad, scale_grad)


def solution(mesh):
    tensor_size, rows_size = mesh.devices.shape
    far = 2
    core = 2
    near = 2
    fine = Mesh(
        mesh.devices.reshape(far, tensor_size // (far * core), core, near, rows_size // near),
        ("xh", "z", "c", "xl", "y"),
    )
    return jax.shard_map(
        per_device,
        mesh=fine,
        in_specs=(
            P(ROWS, None, TENSOR),
            P(None, None, TENSOR),
            P(TENSOR),
            P(),
            P(),
            P(ROWS, TENSOR),
            P(TENSOR),
            P(TENSOR, ROWS),
            P(TENSOR),
            P(TENSOR),
            P(ROWS, None, TENSOR),
        ),
        out_specs=(
            P(ROWS, None, TENSOR),
            P(ROWS, None, TENSOR),
            P(ROWS, TENSOR),
            P(TENSOR, ROWS),
            P(None, None, TENSOR),
            P(TENSOR),
        ),
        check_vma=False,
    )
```
